128 devices in a mesh: batch: 16 (over z, y_hi, core), tm: 8 (over y_lo, x).
Axes of the slice: x: 4, y: 4 (y_hi: 2, y_lo: 2; y = y_hi * 2 + y_lo), z: 4, core: 2. Of those that a mesh axis runs over, the one named last changes fastest.
Arguments:
- x_in: bfloat16 [16, 16, 256, 1280], P('batch', 'tm'), may hold values from -6 to 6
- norm_gain: float32 [1280], replicated, may hold values from 0.5 to 1.5
- w_query: bfloat16 [1280, 640], replicated, may hold values from -1 to 1
- w_key: bfloat16 [1280, 640], replicated, may hold values from -16 to 16
- w_value: bfloat16 [1280, 640], replicated, may hold values from -0.15625 to 0.15625
- w_out: bfloat16 [640, 1280], replicated, may hold values from -0.25 to 0.25
- w_time: bfloat16 [1280, 3, 1280], replicated, may hold values from -0.09375 to 0.09375
- cotangent: bfloat16 [16, 16, 256, 1280], P('batch', 'tm'), may hold values from -6 to 6
Outputs:
- output: bfloat16 [16, 16, 256, 1280], P('batch', 'tm')
- grad_input: bfloat16 [16, 16, 256, 1280], P('batch', 'tm')
- grad_query: float32 [1280, 640], P(('batch', 'tm'))
- grad_key: float32 [1280, 640], P(('batch', 'tm'))
- grad_value: float32 [1280, 640], P(('batch', 'tm'))
- grad_out: float32 [640, 1280], P(('batch', 'tm'))
- grad_gain: float32 [1280], P(('batch', 'tm'))
The draws below stay inside these ranges and needn't reach their ends.
All inputs are finite; a program needn't handle non-finite values.
Results may differ from the reference program's by a relative error of at most 0.014.
The reference program's roundings to bfloat16 on the way count: a program that leaves them out, or rounds other values in their place, can miss the bound.
Values may be sent and summed in bfloat16 or wider, within the bound.
No kernel may reach another device: no remote copies, remote signals or barrier semaphores. Data moves between devices by JAX's collectives and lax.ppermute only.
A program may use at most 192 MiB of HBM per device.

```python
import jax
import jax.numpy as jnp
from jax import lax

C = 1280
HEADS = 10
HD = 64
S = 256
INNER = 640
FRAMES = 16
CLIPS = 16


def weight_pair(key):
    base = jax.random.normal(jax.random.fold_in(key, 11), (C, HEADS * HD), jnp.float32)
    noise = jax.random.normal(jax.random.fold_in(key, 12), (C, HEADS * HD), jnp.float32)
    base = jnp.clip(base, -5.0, 5.0) * C ** (-0.5)
    noise = jnp.clip(noise, -5.0, 5.0) * C ** (-0.5)
    return (base, noise)


def draw_w_query(key, part):
    return weight_pair(key)[0].astype(jnp.bfloat16)


def draw_w_key(key, part):
    return weight_pair(key)[1].astype(jnp.bfloat16)


def steps_of(own_key, shape, cuts, low, largest):
    factor_of = 1.0
    for axis_at, blocks in cuts:
        draws = jax.random.uniform(jax.random.fold_in(jax.random.fold_in(own_key, 6), axis_at), (blocks,), jnp.float32, low / len(cuts), largest / len(cuts))
        factor_of = factor_of * jnp.repeat(jnp.exp(draws), shape[axis_at] // blocks).reshape((-1,) + (1,) * (len(shape) - 1 - axis_at))
    return factor_of


def scatter_about(stream_key, shape, scale, bound, cuts=(), dtype=jnp.bfloat16):
    drawn = scale * jax.random.normal(stream_key, shape, jnp.float32)
    if cuts:
        drawn = drawn * steps_of(stream_key, shape, cuts, -0.22, 0.18)
    return jnp.clip(drawn, -bound, bound).astype(dtype)


def setup_inputs(seed: int = 0) -> dict:
    streams_of = jax.random.split(jax.random.key(seed), 9)
    x_in = scatter_about(streams_of[0], (CLIPS, FRAMES, S, C), 1.0, 6.0, ((0, 16), (1, 8)))
    norm_gain = jnp.clip(1.0 + 0.1 * jax.random.normal(streams_of[1], (C,), jnp.float32), 0.5, 1.5)
    w_query = draw_w_query(jax.random.fold_in(streams_of[8], 71), 0)
    w_key = draw_w_key(jax.random.fold_in(streams_of[8], 71), 0)
    w_value = scatter_about(streams_of[4], (C, INNER), C ** -0.5, 0.15625)
    w_out = scatter_about(streams_of[5], (INNER, C), INNER ** -0.5, 0.25)
    w_time = scatter_about(streams_of[6], (C, 3, C), (3 * C) ** -0.5, 0.09375)
    cotangent = scatter_about(streams_of[7], (CLIPS, FRAMES, S, C), 1.0, 6.0, ((0, 16), (1, 8)))
    return {"x_in": x_in, "norm_gain": norm_gain, "w_query": w_query, "w_key": w_key, "w_value": w_value, "w_out": w_out, "w_time": w_time, "cotangent": cotangent}


eps_norm = 1e-05
highest = lax.Precision.HIGHEST

def layer_norm(inputs, norm_gain):
    wide = inputs.astype(jnp.float32)
    centre = lax.optimization_barrier(jnp.mean(wide, axis=-1, keepdims=True))
    spread = lax.optimization_barrier(jnp.mean((wide - centre) ** 2, axis=-1, keepdims=True))
    inv_std = lax.rsqrt(spread + eps_norm)
    x_hat = (wide - centre) * inv_std
    return ((x_hat * norm_gain).astype(jnp.bfloat16), x_hat, inv_std)

def project(inputs, matrix):
    return jnp.dot(inputs, matrix, preferred_element_type=jnp.float32).astype(jnp.bfloat16)

def split_heads(tensor):
    return tensor.reshape(tensor.shape[:-1] + (HEADS, HD)).astype(jnp.float32)

def attend(queries, key_rows, val_rows, key_first, val_first):
    key_all = jnp.concatenate([key_rows, jnp.broadcast_to(key_first[:, None], key_rows.shape)], axis=2)
    val_all = jnp.concatenate([val_rows, jnp.broadcast_to(val_first[:, None], val_rows.shape)], axis=2)
    scores = jnp.einsum('lfshd,lfthd->lfhst', split_heads(queries), split_heads(key_all)) * HD ** (-0.5)
    top_score = lax.optimization_barrier(jnp.max(scores, axis=-1, keepdims=True))
    expd = jnp.exp(scores - top_score)
    prob_f32 = expd / lax.optimization_barrier(jnp.sum(expd, axis=-1, keepdims=True))
    prob_b = prob_f32.astype(jnp.bfloat16)
    mixed = jnp.einsum('lfhst,lfthd->lfshd', prob_b.astype(jnp.float32), split_heads(val_all))
    attended = mixed.reshape(queries.shape).astype(jnp.bfloat16)
    return (attended, prob_f32, prob_b, key_all, val_all)

def attend_back(grad_att, queries, key_all, val_all, prob_f32, prob_b):
    grad_heads = split_heads(grad_att)
    grad_prob = jnp.einsum('lfshd,lfthd->lfhst', grad_heads, split_heads(val_all))
    centre = lax.optimization_barrier(jnp.sum(grad_prob * prob_f32, axis=-1, keepdims=True))
    grad_score = (prob_f32 * (grad_prob - centre) * HD ** (-0.5)).astype(jnp.bfloat16).astype(jnp.float32)
    grad_queries = jnp.einsum('lfhst,lfthd->lfshd', grad_score, split_heads(key_all))
    grad_queries = grad_queries.reshape(queries.shape).astype(jnp.bfloat16)
    grad_keys = jnp.einsum('lfhst,lfshd->lfthd', grad_score, split_heads(queries)).reshape(key_all.shape)
    grad_vals = jnp.einsum('lfhst,lfshd->lfthd', prob_b.astype(jnp.float32), grad_heads).reshape(val_all.shape)
    frame_len = queries.shape[2]
    return (grad_queries, grad_keys[:, :, :frame_len], grad_vals[:, :, :frame_len], lax.optimization_barrier(jnp.sum(grad_keys[:, :, frame_len:], axis=1)), lax.optimization_barrier(jnp.sum(grad_vals[:, :, frame_len:], axis=1)))

def gram_rows(left, right, precision=None):
    flat_left = left.reshape(-1, left.shape[-1])
    flat_right = right.reshape(-1, right.shape[-1])
    return lax.dot_general(flat_left, flat_right, (((0,), (0,)), ((), ())), preferred_element_type=jnp.float32, precision=precision)

def silu_slope(hidden_wide):
    sigma = jax.nn.sigmoid(hidden_wide)
    return sigma * (1.0 + hidden_wide * (1.0 - sigma))

def time_stack(padded, frames):
    return jnp.stack([padded[:, 0:frames], padded[:, 1:frames + 1], padded[:, 2:frames + 2]], axis=3)

def first_terms(normed_first, key_grad, val_grad, key_wide, val_wide):
    rows = jnp.einsum('lsh,ch->lsc', key_grad, key_wide, precision=highest)
    rows = rows + jnp.einsum('lsh,ch->lsc', val_grad, val_wide, precision=highest)
    extra_key = gram_rows(normed_first.astype(jnp.float32), key_grad, highest)
    extra_val = gram_rows(normed_first.astype(jnp.float32), val_grad, highest)
    return (rows, extra_key, extra_val)

def clip_pass(x_clip, grad_clip, norm_gain, w_query, w_key, w_value, w_out, w_time):
    frames = x_clip.shape[1]
    normed, x_hat, inv_std = layer_norm(x_clip, norm_gain)
    queries = project(normed, w_query)
    key_rows = project(normed, w_key)
    val_rows = project(normed, w_value)
    attended, prob_f32, prob_b, key_all, val_all = attend(queries, key_rows, val_rows, key_rows[:, 0], val_rows[:, 0])
    hidden = (x_clip.astype(jnp.float32) + jnp.dot(attended, w_out, preferred_element_type=jnp.float32)).astype(jnp.bfloat16)
    active = jax.nn.silu(hidden.astype(jnp.float32)).astype(jnp.bfloat16)
    widths = ((0, 0), (1, 1), (0, 0), (0, 0))
    act_pad = jnp.pad(active, widths)
    grad_pad = jnp.pad(grad_clip, widths)
    act_stack = time_stack(act_pad, frames).astype(jnp.float32)
    time_wide = w_time.astype(jnp.float32)
    conv = jnp.einsum('lfsjc,cjo->lfso', act_stack, time_wide)
    output = (hidden.astype(jnp.float32) + conv).astype(jnp.bfloat16)
    grad_stack = jnp.stack([grad_pad[:, 2:frames + 2], grad_pad[:, 1:frames + 1], grad_pad[:, 0:frames]], axis=3)
    grad_act = jnp.einsum('lfsjo,cjo->lfsc', grad_stack.astype(jnp.float32), time_wide)
    grad_hidden = (grad_clip.astype(jnp.float32) + grad_act * silu_slope(hidden.astype(jnp.float32))).astype(jnp.bfloat16)
    grad_out = gram_rows(attended, grad_hidden)
    grad_att = jnp.einsum('lfso,ho->lfsh', grad_hidden.astype(jnp.float32), w_out.astype(jnp.float32)).astype(jnp.bfloat16)
    grad_queries, key_own, val_own, key_first_grad, val_first_grad = attend_back(grad_att, queries, key_all, val_all, prob_f32, prob_b)
    key_b = key_own.astype(jnp.bfloat16)
    val_b = val_own.astype(jnp.bfloat16)
    grad_normed = jnp.dot(grad_queries, w_query.T, preferred_element_type=jnp.float32)
    grad_normed = grad_normed + jnp.dot(key_b, w_key.T, preferred_element_type=jnp.float32)
    grad_normed = grad_normed + jnp.dot(val_b, w_value.T, preferred_element_type=jnp.float32)
    first_rows, extra_key, extra_val = first_terms(normed[:, 0], key_first_grad, val_first_grad, w_key.astype(jnp.float32), w_value.astype(jnp.float32))
    grad_normed = grad_normed.at[:, 0].add(first_rows)
    grad_wq = gram_rows(normed, grad_queries)
    grad_wk = gram_rows(normed, key_b) + extra_key
    grad_wv = gram_rows(normed, val_b) + extra_val
    grad_gain = lax.optimization_barrier(jnp.sum(grad_normed * x_hat, axis=(0, 1, 2)))
    grad_hat = grad_normed * norm_gain
    grad_x = inv_std * (grad_hat - lax.optimization_barrier(jnp.mean(grad_hat, axis=-1, keepdims=True)) - x_hat * lax.optimization_barrier(jnp.mean(grad_hat * x_hat, axis=-1, keepdims=True)))
    grad_input = (grad_hidden.astype(jnp.float32) + grad_x).astype(jnp.bfloat16)
    return (output, grad_input, (grad_wq, grad_wk, grad_wv, grad_out, grad_gain))

def reference(x_in, norm_gain, w_query, w_key, w_value, w_out, w_time, cotangent):
    inner_width = HEADS * HD
    width = x_in.shape[-1]
    start = (jnp.zeros((width, inner_width), jnp.float32), jnp.zeros((width, inner_width), jnp.float32), jnp.zeros((width, inner_width), jnp.float32), jnp.zeros((inner_width, width), jnp.float32), jnp.zeros((width,), jnp.float32))

    def step(totals, pair):
        x_clip, grad_clip = pair
        output, grad_input, grads = clip_pass(x_clip[None], grad_clip[None], norm_gain, w_query, w_key, w_value, w_out, w_time)
        totals = jax.tree.map(lambda left, right: left + right, totals, grads)
        return (totals, (output[0], grad_input[0]))
    totals, outs = lax.scan(step, start, (x_in, cotangent))
    return (outs[0], outs[1], totals[0], totals[1], totals[2], totals[3], totals[4])
```

```python
import functools

import jax
import jax.numpy as jnp
from jax import lax
from jax.sharding import PartitionSpec as P

HEADS = 10
HD = 64


eps_norm = 1e-05
highest = lax.Precision.HIGHEST


def tree_broadcast(block, axis):
    index = lax.axis_index(axis)
    have = block
    for pairs in (((0, 4),), ((0, 3), (4, 7)), ((0, 1), (3, 2), (4, 5), (7, 6))):
        got = lax.ppermute(have, axis, list(pairs))
        hit = functools.reduce(jnp.logical_or, [index == dst for _, dst in pairs])
        have = jnp.where(hit, got, have)
    return have


def tree_reduce(block, axis):
    index = lax.axis_index(axis)
    total = block
    for pairs in (((1, 0), (2, 3), (5, 4), (6, 7)), ((3, 0), (7, 4)), ((4, 0),)):
        got = lax.ppermute(total.astype(jnp.bfloat16), axis, list(pairs))
        hit = functools.reduce(jnp.logical_or, [index == dst for _, dst in pairs])
        total = jnp.where(hit, total + got.astype(jnp.float32), total)
    return total


def scatter_sum(parts, outer, inner):
    count = lax.axis_size(outer) * lax.axis_size(inner)
    packed = jnp.concatenate([p.reshape(count, -1) for p in parts], axis=1)
    share = packed.reshape((lax.axis_size(outer), -1) + packed.shape[1:])
    share = lax.psum_scatter(share, outer, scatter_dimension=0, tiled=True)[0]
    share = lax.all_to_all(share, inner, 0, 0, tiled=True)
    share = jnp.sum(share, axis=0)
    outs, start = [], 0
    for p in parts:
        width = p.size // count
        outs.append(share[start : start + width].reshape((p.shape[0] // count,) + p.shape[1:]))
        start += width
    return outs


def padded_2(value, sides, width):
    for axis, dim in sides:
        size, length = (lax.axis_size(axis), value.shape[dim])
        up = [(i, (i + 1) % size) for i in range(size - 1)]
        down = [(j, i) for i, j in up]
        last = lax.slice_in_dim(value, length - width, length, axis=dim)
        leading = lax.slice_in_dim(value, 0, width, axis=dim)
        before = lax.ppermute(last, axis, up)
        after = lax.ppermute(leading, axis, down)
        value = jnp.concatenate([before, value, after], axis=dim)
    return value


def layer_norm(inputs, norm_gain):
    wide = inputs.astype(jnp.float32)
    centre = jnp.mean(wide, axis=-1, keepdims=True)
    spread = jnp.mean((wide - centre) ** 2, axis=-1, keepdims=True)
    inv_std = lax.rsqrt(spread + eps_norm)
    x_hat = (wide - centre) * inv_std
    return ((x_hat * norm_gain).astype(jnp.bfloat16), x_hat, inv_std)


def project(inputs, matrix):
    return jnp.dot(inputs, matrix, preferred_element_type=jnp.float32).astype(jnp.bfloat16)


def split_heads(tensor):
    return tensor.reshape(tensor.shape[:-1] + (HEADS, HD))


def attend(queries, key_rows, val_rows, key_first, val_first):
    key_all = jnp.concatenate(
        [key_rows, jnp.broadcast_to(key_first[:, None], key_rows.shape)], axis=2
    )
    val_all = jnp.concatenate(
        [val_rows, jnp.broadcast_to(val_first[:, None], val_rows.shape)], axis=2
    )
    scores = jnp.einsum(
        "lfshd,lfthd->lfhst",
        split_heads(queries),
        split_heads(key_all),
        preferred_element_type=jnp.float32,
    ) * HD ** (-0.5)
    top_score = jnp.max(scores, axis=-1, keepdims=True)
    expd = jnp.exp(scores - top_score)
    prob_f32 = expd / jnp.sum(expd, axis=-1, keepdims=True)
    prob_b = prob_f32.astype(jnp.bfloat16)
    mixed = jnp.einsum(
        "lfhst,lfthd->lfshd", prob_b, split_heads(val_all), preferred_element_type=jnp.float32
    )
    attended = mixed.reshape(queries.shape).astype(jnp.bfloat16)
    return (attended, prob_f32, prob_b, key_all, val_all)


def attend_back(grad_att, queries, key_all, val_all, prob_f32, prob_b):
    grad_heads = split_heads(grad_att)
    grad_prob = jnp.einsum(
        "lfshd,lfthd->lfhst", grad_heads, split_heads(val_all), preferred_element_type=jnp.float32
    )
    centre = jnp.sum(grad_prob * prob_f32, axis=-1, keepdims=True)
    grad_score = (prob_f32 * (grad_prob - centre) * HD ** (-0.5)).astype(jnp.bfloat16)
    grad_queries = jnp.einsum(
        "lfhst,lfthd->lfshd", grad_score, split_heads(key_all), preferred_element_type=jnp.float32
    )
    grad_queries = grad_queries.reshape(queries.shape).astype(jnp.bfloat16)
    grad_keys = jnp.einsum(
        "lfhst,lfshd->lfthd", grad_score, split_heads(queries), preferred_element_type=jnp.float32
    ).reshape(key_all.shape)
    grad_vals = jnp.einsum(
        "lfhst,lfshd->lfthd", prob_b, grad_heads, preferred_element_type=jnp.float32
    ).reshape(val_all.shape)
    frame_len = queries.shape[2]
    return (
        grad_queries,
        grad_keys[:, :, :frame_len],
        grad_vals[:, :, :frame_len],
        jnp.sum(grad_keys[:, :, frame_len:], axis=1),
        jnp.sum(grad_vals[:, :, frame_len:], axis=1),
    )


def gram_rows(left, right, precision=None):
    flat_left = left.reshape(-1, left.shape[-1])
    flat_right = right.reshape(-1, right.shape[-1])
    return lax.dot_general(
        flat_left,
        flat_right,
        (((0,), (0,)), ((), ())),
        preferred_element_type=jnp.float32,
        precision=precision,
    )


def silu_slope(hidden_wide):
    sigma = jax.nn.sigmoid(hidden_wide)
    return sigma * (1.0 + hidden_wide * (1.0 - sigma))


def time_stack(padded, frames):
    return jnp.stack(
        [padded[:, 0:frames], padded[:, 1 : frames + 1], padded[:, 2 : frames + 2]], axis=3
    )


def first_terms(normed_first, key_grad, val_grad, key_wide, val_wide):
    rows = jnp.einsum("lsh,ch->lsc", key_grad, key_wide, precision=highest)
    rows = rows + jnp.einsum("lsh,ch->lsc", val_grad, val_wide, precision=highest)
    extra_key = gram_rows(normed_first.astype(jnp.float32), key_grad, highest)
    extra_val = gram_rows(normed_first.astype(jnp.float32), val_grad, highest)
    return (rows, extra_key, extra_val)


def on_device(x_in, norm_gain, w_query, w_key, w_value, w_out, w_time, cotangent):
    frames = x_in.shape[1]
    is_owner = lax.axis_index("tm") == 0
    normed, x_hat, inv_std = layer_norm(x_in, norm_gain)
    queries = project(normed, w_query)
    key_rows = project(normed, w_key)
    val_rows = project(normed, w_value)
    x_first = tree_broadcast(x_in[:, 0], "tm")
    normed_first = layer_norm(x_first, norm_gain)[0]
    key_first = project(normed_first, w_key)
    val_first = project(normed_first, w_value)
    attended, prob_f32, prob_b, key_all, val_all = attend(
        queries, key_rows, val_rows, key_first, val_first
    )
    hidden = (
        x_in.astype(jnp.float32) + jnp.dot(attended, w_out, preferred_element_type=jnp.float32)
    ).astype(jnp.bfloat16)
    active = jax.nn.silu(hidden.astype(jnp.float32)).astype(jnp.bfloat16)
    grad_pad = padded_2(cotangent, (("tm", 1),), 1)
    act_stack = time_stack(padded_2(active, (("tm", 1),), 1), frames)
    conv = jnp.einsum("lfsjc,cjo->lfso", act_stack, w_time, preferred_element_type=jnp.float32)
    output = (hidden.astype(jnp.float32) + conv).astype(jnp.bfloat16)
    grad_stack = jnp.stack(
        [grad_pad[:, 2 : frames + 2], grad_pad[:, 1 : frames + 1], grad_pad[:, 0:frames]], axis=3
    )
    grad_act = jnp.einsum("lfsjo,cjo->lfsc", grad_stack, w_time, preferred_element_type=jnp.float32)
    grad_hidden = (
        cotangent.astype(jnp.float32) + grad_act * silu_slope(hidden.astype(jnp.float32))
    ).astype(jnp.bfloat16)
    grad_out = gram_rows(attended, grad_hidden)
    grad_att = jnp.einsum(
        "lfso,ho->lfsh", grad_hidden, w_out, preferred_element_type=jnp.float32
    ).astype(jnp.bfloat16)
    grad_queries, key_own, val_own, key_first_grad, val_first_grad = attend_back(
        grad_att, queries, key_all, val_all, prob_f32, prob_b
    )
    key_b = key_own.astype(jnp.bfloat16)
    val_b = val_own.astype(jnp.bfloat16)
    grad_normed = jnp.einsum(
        "lfsh,ch->lfsc", grad_queries, w_query, preferred_element_type=jnp.float32
    )
    grad_normed = grad_normed + jnp.einsum(
        "lfsh,ch->lfsc", key_b, w_key, preferred_element_type=jnp.float32
    )
    grad_normed = grad_normed + jnp.einsum(
        "lfsh,ch->lfsc", val_b, w_value, preferred_element_type=jnp.float32
    )
    key_wide = w_key.astype(jnp.float32)
    val_wide = w_value.astype(jnp.float32)
    first_sum = tree_reduce(jnp.concatenate([key_first_grad, val_first_grad], axis=-1), "tm")
    width = key_first_grad.shape[-1]

    def owner_terms(operands):
        rows = jnp.einsum("lsh,ch->lsc", operands[..., :width], key_wide, precision=highest)
        return rows + jnp.einsum("lsh,ch->lsc", operands[..., width:], val_wide, precision=highest)

    def no_terms(operands):
        return jnp.zeros(normed_first.shape, jnp.float32)

    first_rows = lax.cond(is_owner, owner_terms, no_terms, first_sum)
    extra_key = gram_rows(normed_first.astype(jnp.float32), key_first_grad, highest)
    extra_val = gram_rows(normed_first.astype(jnp.float32), val_first_grad, highest)
    grad_normed = grad_normed.at[:, 0].add(first_rows)
    grad_wq = gram_rows(normed, grad_queries)
    grad_wk = gram_rows(normed, key_b) + extra_key
    grad_wv = gram_rows(normed, val_b) + extra_val
    grad_gain = jnp.sum(grad_normed * x_hat, axis=(0, 1, 2))
    grad_hat = grad_normed * norm_gain
    grad_x = inv_std * (
        grad_hat
        - jnp.mean(grad_hat, axis=-1, keepdims=True)
        - x_hat * jnp.mean(grad_hat * x_hat, axis=-1, keepdims=True)
    )
    grad_input = (grad_hidden.astype(jnp.float32) + grad_x).astype(jnp.bfloat16)
    grad_wq, grad_wk, grad_wv, grad_out, grad_gain = scatter_sum(
        (grad_wq, grad_wk, grad_wv, grad_out, grad_gain), "batch", "tm"
    )
    return (output, grad_input, grad_wq, grad_wk, grad_wv, grad_out, grad_gain)


def solution(mesh):
    in_specs = (
        P("batch", "tm", None, None),
        P(),
        P(),
        P(),
        P(),
        P(),
        P(),
        P("batch", "tm", None, None),
    )
    out_specs = (
        P("batch", "tm", None, None),
        P("batch", "tm", None, None),
        P(("batch", "tm"), None),
        P(("batch", "tm"), None),
        P(("batch", "tm"), None),
        P(("batch", "tm"), None),
        P(("batch", "tm")),
    )
    return jax.shard_map(
        on_device, mesh=mesh, in_specs=in_specs, out_specs=out_specs, check_vma=False
    )
```

```python
import functools

import jax
import jax.numpy as jnp
from jax import lax
from jax.sharding import PartitionSpec as P

HEADS = 10
HD = 64


eps_norm = 1e-05
highest = lax.Precision.HIGHEST


def from_owner(block, axis):
    index = lax.axis_index(axis)
    have = block
    for target in range(1, lax.axis_size(axis)):
        got = lax.ppermute(block, axis, [(0, target)])
        have = jnp.where(index == target, got, have)
    return have


def to_owner(block, axis):
    total = block
    for source in range(1, lax.axis_size(axis)):
        got = lax.ppermute(block.astype(jnp.bfloat16), axis, [(source, 0)])
        total = total + got.astype(jnp.float32)
    return total


def scatter_sum(value, outer, inner):
    count = lax.axis_size(outer) * lax.axis_size(inner)
    share = value.reshape((lax.axis_size(outer), lax.axis_size(inner), -1) + value.shape[1:])
    share = lax.psum_scatter(share, outer, scatter_dimension=0, tiled=True)[0]
    share = lax.all_to_all(share, inner, 0, 0, tiled=True)
    share = jnp.sum(share, axis=0)
    return share.reshape((value.shape[0] // count,) + value.shape[1:])


def padded_2(value, sides, width):
    for axis, dim in sides:
        size, length = (lax.axis_size(axis), value.shape[dim])
        up = [(i, (i + 1) % size) for i in range(size - 1)]
        down = [(j, i) for i, j in up]
        last = lax.slice_in_dim(value, length - width, length, axis=dim)
        leading = lax.slice_in_dim(value, 0, width, axis=dim)
        before = lax.ppermute(last, axis, up)
        after = lax.ppermute(leading, axis, down)
        value = jnp.concatenate([before, value, after], axis=dim)
    return value


def layer_norm(inputs, norm_gain):
    wide = inputs.astype(jnp.float32)
    centre = jnp.mean(wide, axis=-1, keepdims=True)
    spread = jnp.mean((wide - centre) ** 2, axis=-1, keepdims=True)
    inv_std = lax.rsqrt(spread + eps_norm)
    x_hat = (wide - centre) * inv_std
    return ((x_hat * norm_gain).astype(jnp.bfloat16), x_hat, inv_std)


def project(inputs, matrix):
    return jnp.dot(inputs, matrix, preferred_element_type=jnp.float32).astype(jnp.bfloat16)


def split_heads(tensor):
    return tensor.reshape(tensor.shape[:-1] + (HEADS, HD))


def attend(queries, key_rows, val_rows, key_first, val_first):
    key_all = jnp.concatenate(
        [key_rows, jnp.broadcast_to(key_first[:, None], key_rows.shape)], axis=2
    )
    val_all = jnp.concatenate(
        [val_rows, jnp.broadcast_to(val_first[:, None], val_rows.shape)], axis=2
    )
    scores = jnp.einsum(
        "lfshd,lfthd->lfhst",
        split_heads(queries),
        split_heads(key_all),
        preferred_element_type=jnp.float32,
    ) * HD ** (-0.5)
    top_score = jnp.max(scores, axis=-1, keepdims=True)
    expd = jnp.exp(scores - top_score)
    prob_f32 = expd / jnp.sum(expd, axis=-1, keepdims=True)
    prob_b = prob_f32.astype(jnp.bfloat16)
    mixed = jnp.einsum(
        "lfhst,lfthd->lfshd", prob_b, split_heads(val_all), preferred_element_type=jnp.float32
    )
    attended = mixed.reshape(queries.shape).astype(jnp.bfloat16)
    return (attended, prob_f32, prob_b, key_all, val_all)


def attend_back(grad_att, queries, key_all, val_all, prob_f32, prob_b):
    grad_heads = split_heads(grad_att)
    grad_prob = jnp.einsum(
        "lfshd,lfthd->lfhst", grad_heads, split_heads(val_all), preferred_element_type=jnp.float32
    )
    centre = jnp.sum(grad_prob * prob_f32, axis=-1, keepdims=True)
    grad_score = (prob_f32 * (grad_prob - centre) * HD ** (-0.5)).astype(jnp.bfloat16)
    grad_queries = jnp.einsum(
        "lfhst,lfthd->lfshd", grad_score, split_heads(key_all), preferred_element_type=jnp.float32
    )
    grad_queries = grad_queries.reshape(queries.shape).astype(jnp.bfloat16)
    grad_keys = jnp.einsum(
        "lfhst,lfshd->lfthd", grad_score, split_heads(queries), preferred_element_type=jnp.float32
    ).reshape(key_all.shape)
    grad_vals = jnp.einsum(
        "lfhst,lfshd->lfthd", prob_b, grad_heads, preferred_element_type=jnp.float32
    ).reshape(val_all.shape)
    frame_len = queries.shape[2]
    return (
        grad_queries,
        grad_keys[:, :, :frame_len],
        grad_vals[:, :, :frame_len],
        jnp.sum(grad_keys[:, :, frame_len:], axis=1),
        jnp.sum(grad_vals[:, :, frame_len:], axis=1),
    )


def gram_rows(left, right, precision=None):
    flat_left = left.reshape(-1, left.shape[-1])
    flat_right = right.reshape(-1, right.shape[-1])
    return lax.dot_general(
        flat_left,
        flat_right,
        (((0,), (0,)), ((), ())),
        preferred_element_type=jnp.float32,
        precision=precision,
    )


def silu_slope(hidden_wide):
    sigma = jax.nn.sigmoid(hidden_wide)
    return sigma * (1.0 + hidden_wide * (1.0 - sigma))


def time_stack(padded, frames):
    return jnp.stack(
        [padded[:, 0:frames], padded[:, 1 : frames + 1], padded[:, 2 : frames + 2]], axis=3
    )


def first_terms(normed_first, key_grad, val_grad, key_wide, val_wide):
    rows = jnp.einsum("lsh,ch->lsc", key_grad, key_wide, precision=highest)
    rows = rows + jnp.einsum("lsh,ch->lsc", val_grad, val_wide, precision=highest)
    extra_key = gram_rows(normed_first.astype(jnp.float32), key_grad, highest)
    extra_val = gram_rows(normed_first.astype(jnp.float32), val_grad, highest)
    return (rows, extra_key, extra_val)


def on_device(x_in, norm_gain, w_query, w_key, w_value, w_out, w_time, cotangent):
    frames = x_in.shape[1]
    is_owner = lax.axis_index("tm") == 0
    normed, x_hat, inv_std = layer_norm(x_in, norm_gain)
    queries = project(normed, w_query)
    key_rows = project(normed, w_key)
    val_rows = project(normed, w_value)
    x_first = from_owner(x_in[:, 0], "tm")
    normed_first = layer_norm(x_first, norm_gain)[0]
    key_first = project(normed_first, w_key)
    val_first = project(normed_first, w_value)
    attended, prob_f32, prob_b, key_all, val_all = attend(
        queries, key_rows, val_rows, key_first, val_first
    )
    hidden = (
        x_in.astype(jnp.float32) + jnp.dot(attended, w_out, preferred_element_type=jnp.float32)
    ).astype(jnp.bfloat16)
    active = jax.nn.silu(hidden.astype(jnp.float32)).astype(jnp.bfloat16)
    grad_pad = padded_2(cotangent, (("tm", 1),), 1)
    act_stack = time_stack(padded_2(active, (("tm", 1),), 1), frames)
    conv = jnp.einsum("lfsjc,cjo->lfso", act_stack, w_time, preferred_element_type=jnp.float32)
    output = (hidden.astype(jnp.float32) + conv).astype(jnp.bfloat16)
    grad_stack = jnp.stack(
        [grad_pad[:, 2 : frames + 2], grad_pad[:, 1 : frames + 1], grad_pad[:, 0:frames]], axis=3
    )
    grad_act = jnp.einsum("lfsjo,cjo->lfsc", grad_stack, w_time, preferred_element_type=jnp.float32)
    grad_hidden = (
        cotangent.astype(jnp.float32) + grad_act * silu_slope(hidden.astype(jnp.float32))
    ).astype(jnp.bfloat16)
    grad_out = gram_rows(attended, grad_hidden)
    grad_att = jnp.einsum(
        "lfso,ho->lfsh", grad_hidden, w_out, preferred_element_type=jnp.float32
    ).astype(jnp.bfloat16)
    grad_queries, key_own, val_own, key_first_grad, val_first_grad = attend_back(
        grad_att, queries, key_all, val_all, prob_f32, prob_b
    )
    key_b = key_own.astype(jnp.bfloat16)
    val_b = val_own.astype(jnp.bfloat16)
    grad_normed = jnp.einsum(
        "lfsh,ch->lfsc", grad_queries, w_query, preferred_element_type=jnp.float32
    )
    grad_normed = grad_normed + jnp.einsum(
        "lfsh,ch->lfsc", key_b, w_key, preferred_element_type=jnp.float32
    )
    grad_normed = grad_normed + jnp.einsum(
        "lfsh,ch->lfsc", val_b, w_value, preferred_element_type=jnp.float32
    )
    key_wide = w_key.astype(jnp.float32)
    val_wide = w_value.astype(jnp.float32)
    first_sum = to_owner(jnp.concatenate([key_first_grad, val_first_grad], axis=-1), "tm")
    width = key_first_grad.shape[-1]

    def owner_terms(operands):
        rows = jnp.einsum("lsh,ch->lsc", operands[..., :width], key_wide, precision=highest)
        return rows + jnp.einsum("lsh,ch->lsc", operands[..., width:], val_wide, precision=highest)

    def no_terms(operands):
        return jnp.zeros(normed_first.shape, jnp.float32)

    first_rows = lax.cond(is_owner, owner_terms, no_terms, first_sum)
    extra_key = gram_rows(normed_first.astype(jnp.float32), key_first_grad, highest)
    extra_val = gram_rows(normed_first.astype(jnp.float32), val_first_grad, highest)
    grad_normed = grad_normed.at[:, 0].add(first_rows)
    grad_wq = gram_rows(normed, grad_queries)
    grad_wk = gram_rows(normed, key_b) + extra_key
    grad_wv = gram_rows(normed, val_b) + extra_val
    grad_gain = jnp.sum(grad_normed * x_hat, axis=(0, 1, 2))
    grad_hat = grad_normed * norm_gain
    grad_x = inv_std * (
        grad_hat
        - jnp.mean(grad_hat, axis=-1, keepdims=True)
        - x_hat * jnp.mean(grad_hat * x_hat, axis=-1, keepdims=True)
    )
    grad_input = (grad_hidden.astype(jnp.float32) + grad_x).astype(jnp.bfloat16)
    grad_wq, grad_wk, grad_wv, grad_out = (
        scatter_sum(grad_wq, "batch", "tm"),
        scatter_sum(grad_wk, "batch", "tm"),
        scatter_sum(grad_wv, "batch", "tm"),
        scatter_sum(grad_out, "batch", "tm"),
    )
    grad_gain = scatter_sum(grad_gain, "batch", "tm")
    return (output, grad_input, grad_wq, grad_wk, grad_wv, grad_out, grad_gain)


def solution(mesh):
    in_specs = (
        P("batch", "tm", None, None),
        P(),
        P(),
        P(),
        P(),
        P(),
        P(),
        P("batch", "tm", None, None),
    )
    out_specs = (
        P("batch", "tm", None, None),
        P("batch", "tm", None, None),
        P(("batch", "tm"), None),
        P(("batch", "tm"), None),
        P(("batch", "tm"), None),
        P(("batch", "tm"), None),
        P(("batch", "tm")),
    )
    return jax.shard_map(
        on_device, mesh=mesh, in_specs=in_specs, out_specs=out_specs, check_vma=False
    )
```

```python
import functools

import jax
import jax.numpy as jnp
from jax import lax
from jax.sharding import PartitionSpec as P

HEADS = 10
HD = 64


eps_norm = 1e-05


def from_owner(block, axis):
    index = lax.axis_index(axis)
    have = block
    for target in range(1, lax.axis_size(axis)):
        got = lax.ppermute(block, axis, [(0, target)])
        have = jnp.where(index == target, got, have)
    return have


def to_owner(block, axis):
    total = block
    for source in range(1, lax.axis_size(axis)):
        got = lax.ppermute(block.astype(jnp.bfloat16), axis, [(source, 0)])
        total = total + got.astype(jnp.float32)
    return total


def scatter_sum(parts, outer, inner):
    count = lax.axis_size(outer) * lax.axis_size(inner)
    packed = jnp.concatenate([p.reshape(count, -1) for p in parts], axis=1)
    share = packed.reshape((lax.axis_size(outer), lax.axis_size(inner), -1))
    share = lax.psum_scatter(share, inner, scatter_dimension=1, tiled=True)
    share = lax.all_to_all(share, outer, 0, 0, tiled=True)
    share = jnp.sum(share, axis=(0, 1))
    outs, start = [], 0
    for p in parts:
        width = p.size // count
        outs.append(share[start : start + width].reshape((p.shape[0] // count,) + p.shape[1:]))
        start += width
    return outs


def split_dot(wide, narrow, dims):
    high = wide.astype(jnp.bfloat16)
    low = (wide - high.astype(jnp.float32)).astype(jnp.bfloat16)
    return sum(
        lax.dot_general(part, narrow, dims, preferred_element_type=jnp.float32)
        for part in (high, low)
    )


def padded_2(value, sides, width):
    for axis, dim in sides:
        size, length = (lax.axis_size(axis), value.shape[dim])
        up = [(i, (i + 1) % size) for i in range(size - 1)]
        down = [(j, i) for i, j in up]
        last = lax.slice_in_dim(value, length - width, length, axis=dim)
        leading = lax.slice_in_dim(value, 0, width, axis=dim)
        before = lax.ppermute(last, axis, up)
        after = lax.ppermute(leading, axis, down)
        value = jnp.concatenate([before, value, after], axis=dim)
    return value


def layer_norm(inputs, norm_gain):
    wide = inputs.astype(jnp.float32)
    centre = jnp.mean(wide, axis=-1, keepdims=True)
    spread = jnp.mean((wide - centre) ** 2, axis=-1, keepdims=True)
    inv_std = lax.rsqrt(spread + eps_norm)
    x_hat = (wide - centre) * inv_std
    return ((x_hat * norm_gain).astype(jnp.bfloat16), x_hat, inv_std)


def project(inputs, matrix):
    return jnp.dot(inputs, matrix, preferred_element_type=jnp.float32).astype(jnp.bfloat16)


def split_heads(tensor):
    return tensor.reshape(tensor.shape[:-1] + (HEADS, HD))


def attend(queries, key_rows, val_rows, key_first, val_first):
    key_all = jnp.concatenate(
        [key_rows, jnp.broadcast_to(key_first[:, None], key_rows.shape)], axis=2
    )
    val_all = jnp.concatenate(
        [val_rows, jnp.broadcast_to(val_first[:, None], val_rows.shape)], axis=2
    )
    scores = jnp.einsum(
        "lfshd,lfthd->lfhst",
        split_heads(queries),
        split_heads(key_all),
        preferred_element_type=jnp.float32,
    ) * HD ** (-0.5)
    top_score = jnp.max(scores, axis=-1, keepdims=True)
    expd = jnp.exp(scores - top_score)
    prob_f32 = expd / jnp.sum(expd, axis=-1, keepdims=True)
    prob_b = prob_f32.astype(jnp.bfloat16)
    mixed = jnp.einsum(
        "lfhst,lfthd->lfshd", prob_b, split_heads(val_all), preferred_element_type=jnp.float32
    )
    attended = mixed.reshape(queries.shape).astype(jnp.bfloat16)
    return (attended, prob_f32, prob_b, key_all, val_all)


def attend_back(grad_att, queries, key_all, val_all, prob_f32, prob_b):
    grad_heads = split_heads(grad_att)
    grad_prob = jnp.einsum(
        "lfshd,lfthd->lfhst", grad_heads, split_heads(val_all), preferred_element_type=jnp.float32
    )
    centre = jnp.sum(grad_prob * prob_f32, axis=-1, keepdims=True)
    grad_score = (prob_f32 * (grad_prob - centre) * HD ** (-0.5)).astype(jnp.bfloat16)
    grad_queries = jnp.einsum(
        "lfhst,lfthd->lfshd", grad_score, split_heads(key_all), preferred_element_type=jnp.float32
    )
    grad_queries = grad_queries.reshape(queries.shape).astype(jnp.bfloat16)
    grad_keys = jnp.einsum(
        "lfhst,lfshd->lfthd", grad_score, split_heads(queries), preferred_element_type=jnp.float32
    ).reshape(key_all.shape)
    grad_vals = jnp.einsum(
        "lfhst,lfshd->lfthd", prob_b, grad_heads, preferred_element_type=jnp.float32
    ).reshape(val_all.shape)
    frame_len = queries.shape[2]
    return (
        grad_queries,
        grad_keys[:, :, :frame_len],
        grad_vals[:, :, :frame_len],
        jnp.sum(grad_keys[:, :, frame_len:], axis=1),
        jnp.sum(grad_vals[:, :, frame_len:], axis=1),
    )


def gram_rows(left, right, precision=None):
    flat_left = left.reshape(-1, left.shape[-1])
    flat_right = right.reshape(-1, right.shape[-1])
    return lax.dot_general(
        flat_left,
        flat_right,
        (((0,), (0,)), ((), ())),
        preferred_element_type=jnp.float32,
        precision=precision,
    )


def silu_slope(hidden_wide):
    sigma = jax.nn.sigmoid(hidden_wide)
    return sigma * (1.0 + hidden_wide * (1.0 - sigma))


def time_stack(padded, frames):
    return jnp.stack(
        [padded[:, 0:frames], padded[:, 1 : frames + 1], padded[:, 2 : frames + 2]], axis=3
    )


def on_device(x_in, norm_gain, w_query, w_key, w_value, w_out, w_time, cotangent):
    frames = x_in.shape[1]
    is_owner = lax.axis_index("tm") == 0
    normed, x_hat, inv_std = layer_norm(x_in, norm_gain)
    queries = project(normed, w_query)
    key_rows = project(normed, w_key)
    val_rows = project(normed, w_value)
    x_first = from_owner(x_in[:, 0], "tm")
    normed_first = layer_norm(x_first, norm_gain)[0]
    key_first = project(normed_first, w_key)
    val_first = project(normed_first, w_value)
    attended, prob_f32, prob_b, key_all, val_all = attend(
        queries, key_rows, val_rows, key_first, val_first
    )
    hidden = (
        x_in.astype(jnp.float32) + jnp.dot(attended, w_out, preferred_element_type=jnp.float32)
    ).astype(jnp.bfloat16)
    active = jax.nn.silu(hidden.astype(jnp.float32)).astype(jnp.bfloat16)
    grad_pad = padded_2(cotangent, (("tm", 1),), 1)
    act_stack = time_stack(padded_2(active, (("tm", 1),), 1), frames)
    conv = jnp.einsum("lfsjc,cjo->lfso", act_stack, w_time, preferred_element_type=jnp.float32)
    output = (hidden.astype(jnp.float32) + conv).astype(jnp.bfloat16)
    grad_stack = jnp.stack(
        [grad_pad[:, 2 : frames + 2], grad_pad[:, 1 : frames + 1], grad_pad[:, 0:frames]], axis=3
    )
    grad_act = jnp.einsum("lfsjo,cjo->lfsc", grad_stack, w_time, preferred_element_type=jnp.float32)
    grad_hidden = (
        cotangent.astype(jnp.float32) + grad_act * silu_slope(hidden.astype(jnp.float32))
    ).astype(jnp.bfloat16)
    grad_out = gram_rows(attended, grad_hidden)
    grad_att = jnp.einsum(
        "lfso,ho->lfsh", grad_hidden, w_out, preferred_element_type=jnp.float32
    ).astype(jnp.bfloat16)
    grad_queries, key_own, val_own, key_first_grad, val_first_grad = attend_back(
        grad_att, queries, key_all, val_all, prob_f32, prob_b
    )
    key_b = key_own.astype(jnp.bfloat16)
    val_b = val_own.astype(jnp.bfloat16)
    grad_normed = jnp.einsum(
        "lfsh,ch->lfsc", grad_queries, w_query, preferred_element_type=jnp.float32
    )
    grad_normed = grad_normed + jnp.einsum(
        "lfsh,ch->lfsc", key_b, w_key, preferred_element_type=jnp.float32
    )
    grad_normed = grad_normed + jnp.einsum(
        "lfsh,ch->lfsc", val_b, w_value, preferred_element_type=jnp.float32
    )
    first_sum = to_owner(jnp.concatenate([key_first_grad, val_first_grad], axis=-1), "tm")
    width = key_first_grad.shape[-1]

    def owner_terms(operands):
        both = jnp.concatenate([w_key, w_value], axis=1)
        return split_dot(operands, both, (((2,), (1,)), ((), ())))

    def no_terms(operands):
        return jnp.zeros(normed_first.shape, jnp.float32)

    first_rows = lax.cond(is_owner, owner_terms, no_terms, first_sum)
    first_flat = normed_first.reshape(-1, normed_first.shape[-1])
    extra_key = split_dot(key_first_grad.reshape(-1, width), first_flat, (((0,), (0,)), ((), ()))).T
    extra_val = split_dot(val_first_grad.reshape(-1, width), first_flat, (((0,), (0,)), ((), ()))).T
    grad_normed = grad_normed.at[:, 0].add(first_rows)
    grad_wq = gram_rows(normed, grad_queries)
    grad_wk = gram_rows(normed, key_b) + extra_key
    grad_wv = gram_rows(normed, val_b) + extra_val
    grad_gain = jnp.sum(grad_normed * x_hat, axis=(0, 1, 2))
    grad_hat = grad_normed * norm_gain
    grad_x = inv_std * (
        grad_hat
        - jnp.mean(grad_hat, axis=-1, keepdims=True)
        - x_hat * jnp.mean(grad_hat * x_hat, axis=-1, keepdims=True)
    )
    grad_input = (grad_hidden.astype(jnp.float32) + grad_x).astype(jnp.bfloat16)
    grad_wq, grad_wk, grad_wv, grad_out, grad_gain = scatter_sum(
        (grad_wq, grad_wk, grad_wv, grad_out, grad_gain), "batch", "tm"
    )
    return (output, grad_input, grad_wq, grad_wk, grad_wv, grad_out, grad_gain)


def solution(mesh):
    in_specs = (
        P("batch", "tm", None, None),
        P(),
        P(),
        P(),
        P(),
        P(),
        P(),
        P("batch", "tm", None, None),
    )
    out_specs = (
        P("batch", "tm", None, None),
        P("batch", "tm", None, None),
        P(("batch", "tm"), None),
        P(("batch", "tm"), None),
        P(("batch", "tm"), None),
        P(("batch", "tm"), None),
        P(("batch", "tm")),
    )
    return jax.shard_map(
        on_device, mesh=mesh, in_specs=in_specs, out_specs=out_specs, check_vma=False
    )
```

```python
import functools

import jax
import jax.numpy as jnp
from jax import lax
from jax.sharding import PartitionSpec as P

HEADS = 10
HD = 64


eps_norm = 1e-05


def from_owner(block, axis):
    index = lax.axis_index(axis)
    have = block
    for target in range(1, lax.axis_size(axis)):
        got = lax.ppermute(block, axis, [(0, target)])
        have = jnp.where(index == target, got, have)
    return have


def to_owner(block, axis):
    total = block
    for source in range(1, lax.axis_size(axis)):
        got = lax.ppermute(block.astype(jnp.bfloat16), axis, [(source, 0)])
        total = total + got.astype(jnp.float32)
    return total


def scatter_sum(parts, outer, inner):
    count = lax.axis_size(outer) * lax.axis_size(inner)
    packed = jnp.concatenate([p.reshape(count, -1) for p in parts], axis=1)
    share = packed.reshape((lax.axis_size(outer), -1) + packed.shape[1:])
    share = lax.psum_scatter(share, outer, scatter_dimension=0, tiled=True)[0]
    share = lax.all_to_all(share, inner, 0, 0, tiled=True)
    share = jnp.sum(share, axis=0)
    outs, start = [], 0
    for p in parts:
        width = p.size // count
        outs.append(share[start : start + width].reshape((p.shape[0] // count,) + p.shape[1:]))
        start += width
    return outs


def split_dot(wide, narrow, dims):
    high = wide.astype(jnp.bfloat16)
    low = (wide - high.astype(jnp.float32)).astype(jnp.bfloat16)
    return sum(
        lax.dot_general(part, narrow, dims, preferred_element_type=jnp.float32)
        for part in (high, low)
    )


def padded_2(value, sides, width):
    for axis, dim in sides:
        size, length = (lax.axis_size(axis), value.shape[dim])
        up = [(i, (i + 1) % size) for i in range(size - 1)]
        down = [(j, i) for i, j in up]
        last = lax.slice_in_dim(value, length - width, length, axis=dim)
        leading = lax.slice_in_dim(value, 0, width, axis=dim)
        before = lax.ppermute(last, axis, up)
        after = lax.ppermute(leading, axis, down)
        value = jnp.concatenate([before, value, after], axis=dim)
    return value


def layer_norm(inputs, norm_gain):
    wide = inputs.astype(jnp.float32)
    centre = jnp.mean(wide, axis=-1, keepdims=True)
    spread = jnp.mean((wide - centre) ** 2, axis=-1, keepdims=True)
    inv_std = lax.rsqrt(spread + eps_norm)
    x_hat = (wide - centre) * inv_std
    return ((x_hat * norm_gain).astype(jnp.bfloat16), x_hat, inv_std)


def project(inputs, matrix):
    return jnp.dot(inputs, matrix, preferred_element_type=jnp.float32).astype(jnp.bfloat16)


def split_heads(tensor):
    return tensor.reshape(tensor.shape[:-1] + (HEADS, HD))


def attend(queries, key_rows, val_rows, key_first, val_first):
    key_all = jnp.concatenate(
        [key_rows, jnp.broadcast_to(key_first[:, None], key_rows.shape)], axis=2
    )
    val_all = jnp.concatenate(
        [val_rows, jnp.broadcast_to(val_first[:, None], val_rows.shape)], axis=2
    )
    scores = jnp.einsum(
        "lfshd,lfthd->lfhst",
        split_heads(queries),
        split_heads(key_all),
        preferred_element_type=jnp.float32,
    ) * HD ** (-0.5)
    top_score = jnp.max(scores, axis=-1, keepdims=True)
    expd = jnp.exp(scores - top_score)
    prob_f32 = expd / jnp.sum(expd, axis=-1, keepdims=True)
    prob_b = prob_f32.astype(jnp.bfloat16)
    mixed = jnp.einsum(
        "lfhst,lfthd->lfshd", prob_b, split_heads(val_all), preferred_element_type=jnp.float32
    )
    attended = mixed.reshape(queries.shape).astype(jnp.bfloat16)
    return (attended, prob_f32, prob_b, key_all, val_all)


def attend_back(grad_att, queries, key_all, val_all, prob_f32, prob_b):
    grad_heads = split_heads(grad_att)
    grad_prob = jnp.einsum(
        "lfshd,lfthd->lfhst", grad_heads, split_heads(val_all), preferred_element_type=jnp.float32
    )
    centre = jnp.sum(grad_prob * prob_f32, axis=-1, keepdims=True)
    grad_score = (prob_f32 * (grad_prob - centre) * HD ** (-0.5)).astype(jnp.bfloat16)
    grad_queries = jnp.einsum(
        "lfhst,lfthd->lfshd", grad_score, split_heads(key_all), preferred_element_type=jnp.float32
    )
    grad_queries = grad_queries.reshape(queries.shape).astype(jnp.bfloat16)
    grad_keys = jnp.einsum(
        "lfhst,lfshd->lfthd", grad_score, split_heads(queries), preferred_element_type=jnp.float32
    ).reshape(key_all.shape)
    grad_vals = jnp.einsum(
        "lfhst,lfshd->lfthd", prob_b, grad_heads, preferred_element_type=jnp.float32
    ).reshape(val_all.shape)
    frame_len = queries.shape[2]
    return (
        grad_queries,
        grad_keys[:, :, :frame_len],
        grad_vals[:, :, :frame_len],
        jnp.sum(grad_keys[:, :, frame_len:], axis=1),
        jnp.sum(grad_vals[:, :, frame_len:], axis=1),
    )


def gram_rows(left, right, precision=None):
    flat_left = left.reshape(-1, left.shape[-1])
    flat_right = right.reshape(-1, right.shape[-1])
    return lax.dot_general(
        flat_left,
        flat_right,
        (((0,), (0,)), ((), ())),
        preferred_element_type=jnp.float32,
        precision=precision,
    )


def silu_slope(hidden_wide):
    sigma = jax.nn.sigmoid(hidden_wide)
    return sigma * (1.0 + hidden_wide * (1.0 - sigma))


def time_stack(padded, frames):
    return jnp.stack(
        [padded[:, 0:frames], padded[:, 1 : frames + 1], padded[:, 2 : frames + 2]], axis=3
    )


def on_device(x_in, norm_gain, w_query, w_key, w_value, w_out, w_time, cotangent):
    frames = x_in.shape[1]
    is_owner = lax.axis_index("tm") == 0
    normed, x_hat, inv_std = layer_norm(x_in, norm_gain)
    queries = project(normed, w_query)
    key_rows = project(normed, w_key)
    val_rows = project(normed, w_value)
    x_first = from_owner(x_in[:, 0], "tm")
    normed_first = layer_norm(x_first, norm_gain)[0]
    key_first = project(normed_first, w_key)
    val_first = project(normed_first, w_value)
    attended, prob_f32, prob_b, key_all, val_all = attend(
        queries, key_rows, val_rows, key_first, val_first
    )
    hidden = (
        x_in.astype(jnp.float32) + jnp.dot(attended, w_out, preferred_element_type=jnp.float32)
    ).astype(jnp.bfloat16)
    active = jax.nn.silu(hidden.astype(jnp.float32)).astype(jnp.bfloat16)
    grad_pad = padded_2(cotangent, (("tm", 1),), 1)
    act_stack = time_stack(padded_2(active, (("tm", 1),), 1), frames)
    conv = jnp.einsum("lfsjc,cjo->lfso", act_stack, w_time, preferred_element_type=jnp.float32)
    output = (hidden.astype(jnp.float32) + conv).astype(jnp.bfloat16)
    grad_stack = jnp.stack(
        [grad_pad[:, 2 : frames + 2], grad_pad[:, 1 : frames + 1], grad_pad[:, 0:frames]], axis=3
    )
    grad_act = jnp.einsum("lfsjo,cjo->lfsc", grad_stack, w_time, preferred_element_type=jnp.float32)
    grad_hidden = (
        cotangent.astype(jnp.float32) + grad_act * silu_slope(hidden.astype(jnp.float32))
    ).astype(jnp.bfloat16)
    grad_out = gram_rows(attended, grad_hidden)
    grad_att = jnp.einsum(
        "lfso,ho->lfsh", grad_hidden, w_out, preferred_element_type=jnp.float32
    ).astype(jnp.bfloat16)
    grad_queries, key_own, val_own, key_first_grad, val_first_grad = attend_back(
        grad_att, queries, key_all, val_all, prob_f32, prob_b
    )
    key_b = key_own.astype(jnp.bfloat16)
    val_b = val_own.astype(jnp.bfloat16)
    grad_normed = jnp.einsum(
        "lfsh,ch->lfsc", grad_queries, w_query, preferred_element_type=jnp.float32
    )
    grad_normed = grad_normed + jnp.einsum(
        "lfsh,ch->lfsc", key_b, w_key, preferred_element_type=jnp.float32
    )
    grad_normed = grad_normed + jnp.einsum(
        "lfsh,ch->lfsc", val_b, w_value, preferred_element_type=jnp.float32
    )
    first_sum = to_owner(jnp.concatenate([key_first_grad, val_first_grad], axis=-1), "tm")
    width = key_first_grad.shape[-1]

    def owner_terms(operands):
        both = jnp.concatenate([w_key, w_value], axis=1)
        return split_dot(operands, both, (((2,), (1,)), ((), ())))

    def no_terms(operands):
        return jnp.zeros(normed_first.shape, jnp.float32)

    first_rows = lax.cond(is_owner, owner_terms, no_terms, first_sum)
    first_flat = normed_first.reshape(-1, normed_first.shape[-1])
    extra_key = split_dot(key_first_grad.reshape(-1, width), first_flat, (((0,), (0,)), ((), ()))).T
    extra_val = split_dot(val_first_grad.reshape(-1, width), first_flat, (((0,), (0,)), ((), ()))).T
    grad_normed = grad_normed.at[:, 0].add(first_rows)
    grad_wq = gram_rows(normed, grad_queries)
    grad_wk = gram_rows(normed, key_b) + extra_key
    grad_wv = gram_rows(normed, val_b) + extra_val
    grad_gain = jnp.sum(grad_normed * x_hat, axis=(0, 1, 2))
    grad_hat = grad_normed * norm_gain
    grad_x = inv_std * (
        grad_hat
        - jnp.mean(grad_hat, axis=-1, keepdims=True)
        - x_hat * jnp.mean(grad_hat * x_hat, axis=-1, keepdims=True)
    )
    grad_input = (grad_hidden.astype(jnp.float32) + grad_x).astype(jnp.bfloat16)
    grad_wq, grad_wk, grad_wv, grad_out, grad_gain = scatter_sum(
        (grad_wq, grad_wk, grad_wv, grad_out, grad_gain), "batch", "tm"
    )
    return (output, grad_input, grad_wq, grad_wk, grad_wv, grad_out, grad_gain)


def solution(mesh):
    in_specs = (
        P("batch", "tm", None, None),
        P(),
        P(),
        P(),
        P(),
        P(),
        P(),
        P("batch", "tm", None, None),
    )
    out_specs = (
        P("batch", "tm", None, None),
        P("batch", "tm", None, None),
        P(("batch", "tm"), None),
        P(("batch", "tm"), None),
        P(("batch", "tm"), None),
        P(("batch", "tm"), None),
        P(("batch", "tm")),
    )
    return jax.shard_map(
        on_device, mesh=mesh, in_specs=in_specs, out_specs=out_specs, check_vma=False
    )
```

```python
import functools

import jax
import jax.numpy as jnp
from jax import lax
from jax.sharding import PartitionSpec as P

HEADS = 10
HD = 64


eps_norm = 1e-05
highest = lax.Precision.HIGHEST


def tree_broadcast(block, axis):
    index = lax.axis_index(axis)
    have = block
    for pairs in (((0, 4),), ((0, 3), (4, 7)), ((0, 1), (3, 2), (4, 5), (7, 6))):
        got = lax.ppermute(have, axis, list(pairs))
        hit = functools.reduce(jnp.logical_or, [index == dst for _, dst in pairs])
        have = jnp.where(hit, got, have)
    return have


def tree_reduce(block, axis):
    index = lax.axis_index(axis)
    total = block
    for pairs in (((1, 0), (2, 3), (5, 4), (6, 7)), ((3, 0), (7, 4)), ((4, 0),)):
        got = lax.ppermute(total.astype(jnp.bfloat16), axis, list(pairs))
        hit = functools.reduce(jnp.logical_or, [index == dst for _, dst in pairs])
        total = jnp.where(hit, total + got.astype(jnp.float32), total)
    return total


def scatter_sum(parts, outer, inner):
    count = lax.axis_size(outer) * lax.axis_size(inner)
    packed = jnp.concatenate([p.reshape(count, -1) for p in parts], axis=1)
    share = packed.reshape((lax.axis_size(outer), -1) + packed.shape[1:])
    share = lax.psum_scatter(share.astype(jnp.bfloat16), outer, scatter_dimension=0, tiled=True)[0]
    share = lax.all_to_all(share.astype(jnp.float32), inner, 0, 0, tiled=True)
    share = jnp.sum(share, axis=0)
    outs, start = [], 0
    for p in parts:
        width = p.size // count
        outs.append(share[start : start + width].reshape((p.shape[0] // count,) + p.shape[1:]))
        start += width
    return outs


def padded_2(value, sides, width):
    for axis, dim in sides:
        size, length = (lax.axis_size(axis), value.shape[dim])
        up = [(i, (i + 1) % size) for i in range(size - 1)]
        down = [(j, i) for i, j in up]
        last = lax.slice_in_dim(value, length - width, length, axis=dim)
        leading = lax.slice_in_dim(value, 0, width, axis=dim)
        before = lax.ppermute(last, axis, up)
        after = lax.ppermute(leading, axis, down)
        value = jnp.concatenate([before, value, after], axis=dim)
    return value


def layer_norm(inputs, norm_gain):
    wide = inputs.astype(jnp.float32)
    centre = jnp.mean(wide, axis=-1, keepdims=True)
    spread = jnp.mean((wide - centre) ** 2, axis=-1, keepdims=True)
    inv_std = lax.rsqrt(spread + eps_norm)
    x_hat = (wide - centre) * inv_std
    return ((x_hat * norm_gain).astype(jnp.bfloat16), x_hat, inv_std)


def project(inputs, matrix):
    return jnp.dot(inputs, matrix, preferred_element_type=jnp.float32).astype(jnp.bfloat16)


def split_heads(tensor):
    return tensor.reshape(tensor.shape[:-1] + (HEADS, HD))


def attend(queries, key_rows, val_rows, key_first, val_first):
    key_all = jnp.concatenate(
        [key_rows, jnp.broadcast_to(key_first[:, None], key_rows.shape)], axis=2
    )
    val_all = jnp.concatenate(
        [val_rows, jnp.broadcast_to(val_first[:, None], val_rows.shape)], axis=2
    )
    scores = jnp.einsum(
        "lfshd,lfthd->lfhst",
        split_heads(queries),
        split_heads(key_all),
        preferred_element_type=jnp.float32,
    ) * HD ** (-0.5)
    top_score = jnp.max(scores, axis=-1, keepdims=True)
    expd = jnp.exp(scores - top_score)
    prob_f32 = expd / jnp.sum(expd, axis=-1, keepdims=True)
    prob_b = prob_f32.astype(jnp.bfloat16)
    mixed = jnp.einsum(
        "lfhst,lfthd->lfshd", prob_b, split_heads(val_all), preferred_element_type=jnp.float32
    )
    attended = mixed.reshape(queries.shape).astype(jnp.bfloat16)
    return (attended, prob_f32, prob_b, key_all, val_all)


def attend_back(grad_att, queries, key_all, val_all, prob_f32, prob_b):
    grad_heads = split_heads(grad_att)
    grad_prob = jnp.einsum(
        "lfshd,lfthd->lfhst", grad_heads, split_heads(val_all), preferred_element_type=jnp.float32
    )
    centre = jnp.sum(grad_prob * prob_f32, axis=-1, keepdims=True)
    grad_score = (prob_f32 * (grad_prob - centre) * HD ** (-0.5)).astype(jnp.bfloat16)
    grad_queries = jnp.einsum(
        "lfhst,lfthd->lfshd", grad_score, split_heads(key_all), preferred_element_type=jnp.float32
    )
    grad_queries = grad_queries.reshape(queries.shape).astype(jnp.bfloat16)
    grad_keys = jnp.einsum(
        "lfhst,lfshd->lfthd", grad_score, split_heads(queries), preferred_element_type=jnp.float32
    ).reshape(key_all.shape)
    grad_vals = jnp.einsum(
        "lfhst,lfshd->lfthd", prob_b, grad_heads, preferred_element_type=jnp.float32
    ).reshape(val_all.shape)
    frame_len = queries.shape[2]
    return (
        grad_queries,
        grad_keys[:, :, :frame_len],
        grad_vals[:, :, :frame_len],
        jnp.sum(grad_keys[:, :, frame_len:], axis=1),
        jnp.sum(grad_vals[:, :, frame_len:], axis=1),
    )


def gram_rows(left, right, precision=None):
    flat_left = left.reshape(-1, left.shape[-1])
    flat_right = right.reshape(-1, right.shape[-1])
    return lax.dot_general(
        flat_left,
        flat_right,
        (((0,), (0,)), ((), ())),
        preferred_element_type=jnp.float32,
        precision=precision,
    )


def silu_slope(hidden_wide):
    sigma = jax.nn.sigmoid(hidden_wide)
    return sigma * (1.0 + hidden_wide * (1.0 - sigma))


def time_stack(padded, frames):
    return jnp.stack(
        [padded[:, 0:frames], padded[:, 1 : frames + 1], padded[:, 2 : frames + 2]], axis=3
    )


def first_terms(normed_first, key_grad, val_grad, key_wide, val_wide):
    rows = jnp.einsum("lsh,ch->lsc", key_grad, key_wide, precision=highest)
    rows = rows + jnp.einsum("lsh,ch->lsc", val_grad, val_wide, precision=highest)
    extra_key = gram_rows(normed_first.astype(jnp.float32), key_grad, highest)
    extra_val = gram_rows(normed_first.astype(jnp.float32), val_grad, highest)
    return (rows, extra_key, extra_val)


def on_device(x_in, norm_gain, w_query, w_key, w_value, w_out, w_time, cotangent):
    frames = x_in.shape[1]
    is_owner = lax.axis_index("tm") == 0
    normed, x_hat, inv_std = layer_norm(x_in, norm_gain)
    queries = project(normed, w_query)
    key_rows = project(normed, w_key)
    val_rows = project(normed, w_value)
    x_first = tree_broadcast(x_in[:, 0], "tm")
    normed_first = layer_norm(x_first, norm_gain)[0]
    key_first = project(normed_first, w_key)
    val_first = project(normed_first, w_value)
    attended, prob_f32, prob_b, key_all, val_all = attend(
        queries, key_rows, val_rows, key_first, val_first
    )
    hidden = (
        x_in.astype(jnp.float32) + jnp.dot(attended, w_out, preferred_element_type=jnp.float32)
    ).astype(jnp.bfloat16)
    active = jax.nn.silu(hidden.astype(jnp.float32)).astype(jnp.bfloat16)
    grad_pad = padded_2(cotangent, (("tm", 1),), 1)
    act_stack = time_stack(padded_2(active, (("tm", 1),), 1), frames)
    conv = jnp.einsum("lfsjc,cjo->lfso", act_stack, w_time, preferred_element_type=jnp.float32)
    output = (hidden.astype(jnp.float32) + conv).astype(jnp.bfloat16)
    grad_stack = jnp.stack(
        [grad_pad[:, 2 : frames + 2], grad_pad[:, 1 : frames + 1], grad_pad[:, 0:frames]], axis=3
    )
    grad_act = jnp.einsum("lfsjo,cjo->lfsc", grad_stack, w_time, preferred_element_type=jnp.float32)
    grad_hidden = (
        cotangent.astype(jnp.float32) + grad_act * silu_slope(hidden.astype(jnp.float32))
    ).astype(jnp.bfloat16)
    grad_out = gram_rows(attended, grad_hidden)
    grad_att = jnp.einsum(
        "lfso,ho->lfsh", grad_hidden, w_out, preferred_element_type=jnp.float32
    ).astype(jnp.bfloat16)
    grad_queries, key_own, val_own, key_first_grad, val_first_grad = attend_back(
        grad_att, queries, key_all, val_all, prob_f32, prob_b
    )
    key_b = key_own.astype(jnp.bfloat16)
    val_b = val_own.astype(jnp.bfloat16)
    grad_normed = jnp.einsum(
        "lfsh,ch->lfsc", grad_queries, w_query, preferred_element_type=jnp.float32
    )
    grad_normed = grad_normed + jnp.einsum(
        "lfsh,ch->lfsc", key_b, w_key, preferred_element_type=jnp.float32
    )
    grad_normed = grad_normed + jnp.einsum(
        "lfsh,ch->lfsc", val_b, w_value, preferred_element_type=jnp.float32
    )
    key_wide = w_key.astype(jnp.float32)
    val_wide = w_value.astype(jnp.float32)
    first_sum = tree_reduce(jnp.concatenate([key_first_grad, val_first_grad], axis=-1), "tm")
    width = key_first_grad.shape[-1]

    def owner_terms(operands):
        rows = jnp.einsum("lsh,ch->lsc", operands[..., :width], key_wide, precision=highest)
        return rows + jnp.einsum("lsh,ch->lsc", operands[..., width:], val_wide, precision=highest)

    def no_terms(operands):
        return jnp.zeros(normed_first.shape, jnp.float32)

    first_rows = lax.cond(is_owner, owner_terms, no_terms, first_sum)
    extra_key = gram_rows(normed_first.astype(jnp.float32), key_first_grad, highest)
    extra_val = gram_rows(normed_first.astype(jnp.float32), val_first_grad, highest)
    grad_normed = grad_normed.at[:, 0].add(first_rows)
    grad_wq = gram_rows(normed, grad_queries)
    grad_wk = gram_rows(normed, key_b) + extra_key
    grad_wv = gram_rows(normed, val_b) + extra_val
    grad_gain = jnp.sum(grad_normed * x_hat, axis=(0, 1, 2))
    grad_hat = grad_normed * norm_gain
    grad_x = inv_std * (
        grad_hat
        - jnp.mean(grad_hat, axis=-1, keepdims=True)
        - x_hat * jnp.mean(grad_hat * x_hat, axis=-1, keepdims=True)
    )
    grad_input = (grad_hidden.astype(jnp.float32) + grad_x).astype(jnp.bfloat16)
    grad_wq, grad_wk, grad_wv, grad_out, grad_gain = scatter_sum(
        (grad_wq, grad_wk, grad_wv, grad_out, grad_gain), "batch", "tm"
    )
    return (output, grad_input, grad_wq, grad_wk, grad_wv, grad_out, grad_gain)


def solution(mesh):
    in_specs = (
        P("batch", "tm", None, None),
        P(),
        P(),
        P(),
        P(),
        P(),
        P(),
        P("batch", "tm", None, None),
    )
    out_specs = (
        P("batch", "tm", None, None),
        P("batch", "tm", None, None),
        P(("batch", "tm"), None),
        P(("batch", "tm"), None),
        P(("batch", "tm"), None),
        P(("batch", "tm"), None),
        P(("batch", "tm")),
    )
    return jax.shard_map(
        on_device, mesh=mesh, in_specs=in_specs, out_specs=out_specs, check_vma=False
    )
```

```python
import functools

import jax
import jax.numpy as jnp
from jax import lax
from jax.sharding import PartitionSpec as P

HEADS = 10
HD = 64


eps_norm = 1e-05


def from_owner(block, axis):
    index = lax.axis_index(axis)
    have = block
    for target in range(1, lax.axis_size(axis)):
        got = lax.ppermute(block, axis, [(0, target)])
        have = jnp.where(index == target, got, have)
    return have


def to_owner(block, axis):
    total = block
    for source in range(1, lax.axis_size(axis)):
        got = lax.ppermute(block.astype(jnp.bfloat16), axis, [(source, 0)])
        total = total + got.astype(jnp.float32)
    return total


def scatter_sum(parts, outer, inner):
    count = lax.axis_size(outer) * lax.axis_size(inner)
    packed = jnp.concatenate([p.reshape(count, -1) for p in parts], axis=1)
    share = packed.reshape((lax.axis_size(outer), -1) + packed.shape[1:])
    share = lax.psum_scatter(share.astype(jnp.bfloat16), outer, scatter_dimension=0, tiled=True)[0]
    share = lax.all_to_all(share.astype(jnp.float32), inner, 0, 0, tiled=True)
    share = jnp.sum(share, axis=0)
    outs, start = [], 0
    for p in parts:
        width = p.size // count
        outs.append(share[start : start + width].reshape((p.shape[0] // count,) + p.shape[1:]))
        start += width
    return outs


def split_dot(wide, narrow, dims):
    high = wide.astype(jnp.bfloat16)
    low = (wide - high.astype(jnp.float32)).astype(jnp.bfloat16)
    return sum(
        lax.dot_general(part, narrow, dims, preferred_element_type=jnp.float32)
        for part in (high, low)
    )


def padded_2(value, sides, width):
    for axis, dim in sides:
        size, length = (lax.axis_size(axis), value.shape[dim])
        up = [(i, (i + 1) % size) for i in range(size - 1)]
        down = [(j, i) for i, j in up]
        last = lax.slice_in_dim(value, length - width, length, axis=dim)
        leading = lax.slice_in_dim(value, 0, width, axis=dim)
        before = lax.ppermute(last, axis, up)
        after = lax.ppermute(leading, axis, down)
        value = jnp.concatenate([before, value, after], axis=dim)
    return value


def layer_norm(inputs, norm_gain):
    wide = inputs.astype(jnp.float32)
    centre = jnp.mean(wide, axis=-1, keepdims=True)
    spread = jnp.mean((wide - centre) ** 2, axis=-1, keepdims=True)
    inv_std = lax.rsqrt(spread + eps_norm)
    x_hat = (wide - centre) * inv_std
    return ((x_hat * norm_gain).astype(jnp.bfloat16), x_hat, inv_std)


def project(inputs, matrix):
    return jnp.dot(inputs, matrix, preferred_element_type=jnp.float32).astype(jnp.bfloat16)


def split_heads(tensor):
    return tensor.reshape(tensor.shape[:-1] + (HEADS, HD))


def attend(queries, key_rows, val_rows, key_first, val_first):
    key_all = jnp.concatenate(
        [key_rows, jnp.broadcast_to(key_first[:, None], key_rows.shape)], axis=2
    )
    val_all = jnp.concatenate(
        [val_rows, jnp.broadcast_to(val_first[:, None], val_rows.shape)], axis=2
    )
    scores = jnp.einsum(
        "lfshd,lfthd->lfhst",
        split_heads(queries),
        split_heads(key_all),
        preferred_element_type=jnp.float32,
    ) * HD ** (-0.5)
    top_score = jnp.max(scores, axis=-1, keepdims=True)
    expd = jnp.exp(scores - top_score)
    prob_f32 = expd / jnp.sum(expd, axis=-1, keepdims=True)
    prob_b = prob_f32.astype(jnp.bfloat16)
    mixed = jnp.einsum(
        "lfhst,lfthd->lfshd", prob_b, split_heads(val_all), preferred_element_type=jnp.float32
    )
    attended = mixed.reshape(queries.shape).astype(jnp.bfloat16)
    return (attended, prob_f32, prob_b, key_all, val_all)


def attend_back(grad_att, queries, key_all, val_all, prob_f32, prob_b):
    grad_heads = split_heads(grad_att)
    grad_prob = jnp.einsum(
        "lfshd,lfthd->lfhst", grad_heads, split_heads(val_all), preferred_element_type=jnp.float32
    )
    centre = jnp.sum(grad_prob * prob_f32, axis=-1, keepdims=True)
    grad_score = (prob_f32 * (grad_prob - centre) * HD ** (-0.5)).astype(jnp.bfloat16)
    grad_queries = jnp.einsum(
        "lfhst,lfthd->lfshd", grad_score, split_heads(key_all), preferred_element_type=jnp.float32
    )
    grad_queries = grad_queries.reshape(queries.shape).astype(jnp.bfloat16)
    grad_keys = jnp.einsum(
        "lfhst,lfshd->lfthd", grad_score, split_heads(queries), preferred_element_type=jnp.float32
    ).reshape(key_all.shape)
    grad_vals = jnp.einsum(
        "lfhst,lfshd->lfthd", prob_b, grad_heads, preferred_element_type=jnp.float32
    ).reshape(val_all.shape)
    frame_len = queries.shape[2]
    return (
        grad_queries,
        grad_keys[:, :, :frame_len],
        grad_vals[:, :, :frame_len],
        jnp.sum(grad_keys[:, :, frame_len:], axis=1),
        jnp.sum(grad_vals[:, :, frame_len:], axis=1),
    )


def gram_rows(left, right, precision=None):
    flat_left = left.reshape(-1, left.shape[-1])
    flat_right = right.reshape(-1, right.shape[-1])
    return lax.dot_general(
        flat_left,
        flat_right,
        (((0,), (0,)), ((), ())),
        preferred_element_type=jnp.float32,
        precision=precision,
    )


def silu_slope(hidden_wide):
    sigma = jax.nn.sigmoid(hidden_wide)
    return sigma * (1.0 + hidden_wide * (1.0 - sigma))


def time_stack(padded, frames):
    return jnp.stack(
        [padded[:, 0:frames], padded[:, 1 : frames + 1], padded[:, 2 : frames + 2]], axis=3
    )


def on_device(x_in, norm_gain, w_query, w_key, w_value, w_out, w_time, cotangent):
    frames = x_in.shape[1]
    is_owner = lax.axis_index("tm") == 0
    normed, x_hat, inv_std = layer_norm(x_in, norm_gain)
    queries = project(normed, w_query)
    key_rows = project(normed, w_key)
    val_rows = project(normed, w_value)
    x_first = from_owner(x_in[:, 0], "tm")
    normed_first = layer_norm(x_first, norm_gain)[0]
    key_first = project(normed_first, w_key)
    val_first = project(normed_first, w_value)
    attended, prob_f32, prob_b, key_all, val_all = attend(
        queries, key_rows, val_rows, key_first, val_first
    )
    hidden = (
        x_in.astype(jnp.float32) + jnp.dot(attended, w_out, preferred_element_type=jnp.float32)
    ).astype(jnp.bfloat16)
    active = jax.nn.silu(hidden.astype(jnp.float32)).astype(jnp.bfloat16)
    grad_pad = padded_2(cotangent, (("tm", 1),), 1)
    act_stack = time_stack(padded_2(active, (("tm", 1),), 1), frames)
    conv = jnp.einsum("lfsjc,cjo->lfso", act_stack, w_time, preferred_element_type=jnp.float32)
    output = (hidden.astype(jnp.float32) + conv).astype(jnp.bfloat16)
    grad_stack = jnp.stack(
        [grad_pad[:, 2 : frames + 2], grad_pad[:, 1 : frames + 1], grad_pad[:, 0:frames]], axis=3
    )
    grad_act = jnp.einsum("lfsjo,cjo->lfsc", grad_stack, w_time, preferred_element_type=jnp.float32)
    grad_hidden = (
        cotangent.astype(jnp.float32) + grad_act * silu_slope(hidden.astype(jnp.float32))
    ).astype(jnp.bfloat16)
    grad_out = gram_rows(attended, grad_hidden)
    grad_att = jnp.einsum(
        "lfso,ho->lfsh", grad_hidden, w_out, preferred_element_type=jnp.float32
    ).astype(jnp.bfloat16)
    grad_queries, key_own, val_own, key_first_grad, val_first_grad = attend_back(
        grad_att, queries, key_all, val_all, prob_f32, prob_b
    )
    key_b = key_own.astype(jnp.bfloat16)
    val_b = val_own.astype(jnp.bfloat16)
    grad_normed = jnp.einsum(
        "lfsh,ch->lfsc", grad_queries, w_query, preferred_element_type=jnp.float32
    )
    grad_normed = grad_normed + jnp.einsum(
        "lfsh,ch->lfsc", key_b, w_key, preferred_element_type=jnp.float32
    )
    grad_normed = grad_normed + jnp.einsum(
        "lfsh,ch->lfsc", val_b, w_value, preferred_element_type=jnp.float32
    )
    first_sum = to_owner(jnp.concatenate([key_first_grad, val_first_grad], axis=-1), "tm")
    width = key_first_grad.shape[-1]

    dims = (((2,), (1,)), ((), ()))
    first_rows = split_dot(first_sum[..., :width], w_key, dims)
    first_rows = first_rows + split_dot(first_sum[..., width:], w_value, dims)
    first_rows = jnp.where(is_owner, first_rows, jnp.zeros_like(first_rows))
    first_flat = normed_first.reshape(-1, normed_first.shape[-1])
    extra_key = split_dot(key_first_grad.reshape(-1, width), first_flat, (((0,), (0,)), ((), ()))).T
    extra_val = split_dot(val_first_grad.reshape(-1, width), first_flat, (((0,), (0,)), ((), ()))).T
    grad_normed = grad_normed.at[:, 0].add(first_rows)
    grad_wq = gram_rows(normed, grad_queries)
    grad_wk = gram_rows(normed, key_b) + extra_key
    grad_wv = gram_rows(normed, val_b) + extra_val
    grad_gain = jnp.sum(grad_normed * x_hat, axis=(0, 1, 2))
    grad_hat = grad_normed * norm_gain
    grad_x = inv_std * (
        grad_hat
        - jnp.mean(grad_hat, axis=-1, keepdims=True)
        - x_hat * jnp.mean(grad_hat * x_hat, axis=-1, keepdims=True)
    )
    grad_input = (grad_hidden.astype(jnp.float32) + grad_x).astype(jnp.bfloat16)
    grad_wq, grad_wk, grad_wv, grad_out, grad_gain = scatter_sum(
        (grad_wq, grad_wk, grad_wv, grad_out, grad_gain), "batch", "tm"
    )
    return (output, grad_input, grad_wq, grad_wk, grad_wv, grad_out, grad_gain)


def solution(mesh):
    in_specs = (
        P("batch", "tm", None, None),
        P(),
        P(),
        P(),
        P(),
        P(),
        P(),
        P("batch", "tm", None, None),
    )
    out_specs = (
        P("batch", "tm", None, None),
        P("batch", "tm", None, None),
        P(("batch", "tm"), None),
        P(("batch", "tm"), None),
        P(("batch", "tm"), None),
        P(("batch", "tm"), None),
        P(("batch", "tm")),
    )
    return jax.shard_map(
        on_device, mesh=mesh, in_specs=in_specs, out_specs=out_specs, check_vma=False
    )
```

```python
import functools

import jax
import jax.numpy as jnp
from jax import lax
from jax.sharding import PartitionSpec as P

HEADS = 10
HD = 64


eps_norm = 1e-05


def from_owner(block, axis):
    index = lax.axis_index(axis)
    have = block
    for target in range(1, lax.axis_size(axis)):
        got = lax.ppermute(block, axis, [(0, target)])
        have = jnp.where(index == target, got, have)
    return have


def to_owner(block, axis):
    total = block
    for source in range(1, lax.axis_size(axis)):
        got = lax.ppermute(block.astype(jnp.bfloat16), axis, [(source, 0)])
        total = total + got.astype(jnp.float32)
    return total


def scatter_sum(parts, outer, inner):
    count = lax.axis_size(outer) * lax.axis_size(inner)
    packed = jnp.concatenate([p.astype(jnp.bfloat16).reshape(count, -1) for p in parts], axis=1)
    share = packed.reshape((lax.axis_size(outer), -1) + packed.shape[1:])
    share = lax.psum_scatter(share, outer, scatter_dimension=0, tiled=True)[0]
    share = lax.all_to_all(share.astype(jnp.float32), inner, 0, 0, tiled=True)
    share = jnp.sum(share, axis=0)
    outs, start = [], 0
    for p in parts:
        width = p.size // count
        outs.append(share[start : start + width].reshape((p.shape[0] // count,) + p.shape[1:]))
        start += width
    return outs


def split_dot(wide, narrow, dims):
    high = wide.astype(jnp.bfloat16)
    low = (wide - high.astype(jnp.float32)).astype(jnp.bfloat16)
    return sum(
        lax.dot_general(part, narrow, dims, preferred_element_type=jnp.float32)
        for part in (high, low)
    )


def padded_2(value, sides, width):
    for axis, dim in sides:
        size, length = (lax.axis_size(axis), value.shape[dim])
        up = [(i, (i + 1) % size) for i in range(size - 1)]
        down = [(j, i) for i, j in up]
        last = lax.slice_in_dim(value, length - width, length, axis=dim)
        leading = lax.slice_in_dim(value, 0, width, axis=dim)
        before = lax.ppermute(last, axis, up)
        after = lax.ppermute(leading, axis, down)
        value = jnp.concatenate([before, value, after], axis=dim)
    return value


def layer_norm(inputs, norm_gain):
    wide = inputs.astype(jnp.float32)
    centre = jnp.mean(wide, axis=-1, keepdims=True)
    spread = jnp.mean((wide - centre) ** 2, axis=-1, keepdims=True)
    inv_std = lax.rsqrt(spread + eps_norm)
    x_hat = (wide - centre) * inv_std
    return ((x_hat * norm_gain).astype(jnp.bfloat16), x_hat, inv_std)


def project(inputs, matrix):
    return jnp.dot(inputs, matrix, preferred_element_type=jnp.float32).astype(jnp.bfloat16)


def split_heads(tensor):
    return tensor.reshape(tensor.shape[:-1] + (HEADS, HD))


def attend(queries, key_rows, val_rows, key_first, val_first):
    key_all = jnp.concatenate(
        [key_rows, jnp.broadcast_to(key_first[:, None], key_rows.shape)], axis=2
    )
    val_all = jnp.concatenate(
        [val_rows, jnp.broadcast_to(val_first[:, None], val_rows.shape)], axis=2
    )
    scores = jnp.einsum(
        "lfshd,lfthd->lfhst",
        split_heads(queries),
        split_heads(key_all),
        preferred_element_type=jnp.float32,
    ) * HD ** (-0.5)
    top_score = jnp.max(scores, axis=-1, keepdims=True)
    expd = jnp.exp(scores - top_score)
    prob_f32 = expd / jnp.sum(expd, axis=-1, keepdims=True)
    prob_b = lax.optimization_barrier(prob_f32.astype(jnp.bfloat16))
    mixed = jnp.einsum(
        "lfhst,lfthd->lfshd", prob_b, split_heads(val_all), preferred_element_type=jnp.float32
    )
    attended = mixed.reshape(queries.shape).astype(jnp.bfloat16)
    return (attended, prob_f32, prob_b, key_all, val_all)


def attend_back(grad_att, queries, key_all, val_all, prob_f32, prob_b):
    grad_heads = split_heads(grad_att)
    grad_prob = jnp.einsum(
        "lfshd,lfthd->lfhst", grad_heads, split_heads(val_all), preferred_element_type=jnp.float32
    )
    centre = jnp.sum(grad_prob * prob_f32, axis=-1, keepdims=True)
    grad_score = (prob_f32 * (grad_prob - centre) * HD ** (-0.5)).astype(jnp.bfloat16)
    grad_score = lax.optimization_barrier(grad_score)
    grad_queries = jnp.einsum(
        "lfhst,lfthd->lfshd", grad_score, split_heads(key_all), preferred_element_type=jnp.float32
    )
    grad_queries = grad_queries.reshape(queries.shape).astype(jnp.bfloat16)
    grad_keys = jnp.einsum(
        "lfhst,lfshd->lfthd", grad_score, split_heads(queries), preferred_element_type=jnp.float32
    ).reshape(key_all.shape)
    grad_vals = jnp.einsum(
        "lfhst,lfshd->lfthd", prob_b, grad_heads, preferred_element_type=jnp.float32
    ).reshape(val_all.shape)
    frame_len = queries.shape[2]
    return (
        grad_queries,
        grad_keys[:, :, :frame_len],
        grad_vals[:, :, :frame_len],
        jnp.sum(grad_keys[:, :, frame_len:], axis=1),
        jnp.sum(grad_vals[:, :, frame_len:], axis=1),
    )


def gram_rows(left, right, precision=None):
    flat_left = left.reshape(-1, left.shape[-1])
    flat_right = right.reshape(-1, right.shape[-1])
    return lax.dot_general(
        flat_left,
        flat_right,
        (((0,), (0,)), ((), ())),
        preferred_element_type=jnp.float32,
        precision=precision,
    )


def silu_slope(hidden_wide):
    sigma = jax.nn.sigmoid(hidden_wide)
    return sigma * (1.0 + hidden_wide * (1.0 - sigma))


def time_stack(padded, frames):
    return jnp.stack(
        [padded[:, 0:frames], padded[:, 1 : frames + 1], padded[:, 2 : frames + 2]], axis=3
    )


def on_device(x_in, norm_gain, w_query, w_key, w_value, w_out, w_time, cotangent):
    frames = x_in.shape[1]
    is_owner = lax.axis_index("tm") == 0
    normed, x_hat, inv_std = layer_norm(x_in, norm_gain)
    queries = project(normed, w_query)
    key_rows = project(normed, w_key)
    val_rows = project(normed, w_value)
    x_first = from_owner(x_in[:, 0], "tm")
    normed_first = layer_norm(x_first, norm_gain)[0]
    key_first = project(normed_first, w_key)
    val_first = project(normed_first, w_value)
    attended, prob_f32, prob_b, key_all, val_all = attend(
        queries, key_rows, val_rows, key_first, val_first
    )
    hidden = (
        x_in.astype(jnp.float32) + jnp.dot(attended, w_out, preferred_element_type=jnp.float32)
    ).astype(jnp.bfloat16)
    active = jax.nn.silu(hidden.astype(jnp.float32)).astype(jnp.bfloat16)
    grad_pad = padded_2(cotangent, (("tm", 1),), 1)
    act_stack = time_stack(padded_2(active, (("tm", 1),), 1), frames)
    conv = jnp.einsum("lfsjc,cjo->lfso", act_stack, w_time, preferred_element_type=jnp.float32)
    output = (hidden.astype(jnp.float32) + conv).astype(jnp.bfloat16)
    grad_stack = jnp.stack(
        [grad_pad[:, 2 : frames + 2], grad_pad[:, 1 : frames + 1], grad_pad[:, 0:frames]], axis=3
    )
    grad_act = jnp.einsum("lfsjo,cjo->lfsc", grad_stack, w_time, preferred_element_type=jnp.float32)
    grad_hidden = (
        cotangent.astype(jnp.float32) + grad_act * silu_slope(hidden.astype(jnp.float32))
    ).astype(jnp.bfloat16)
    grad_out = gram_rows(attended, grad_hidden)
    grad_att = jnp.einsum(
        "lfso,ho->lfsh", grad_hidden, w_out, preferred_element_type=jnp.float32
    ).astype(jnp.bfloat16)
    grad_queries, key_own, val_own, key_first_grad, val_first_grad = attend_back(
        grad_att, queries, key_all, val_all, prob_f32, prob_b
    )
    key_b = key_own.astype(jnp.bfloat16)
    val_b = val_own.astype(jnp.bfloat16)
    grad_normed = jnp.einsum(
        "lfsh,ch->lfsc", grad_queries, w_query, preferred_element_type=jnp.float32
    )
    grad_normed = grad_normed + jnp.einsum(
        "lfsh,ch->lfsc", key_b, w_key, preferred_element_type=jnp.float32
    )
    grad_normed = grad_normed + jnp.einsum(
        "lfsh,ch->lfsc", val_b, w_value, preferred_element_type=jnp.float32
    )
    first_sum = to_owner(jnp.concatenate([key_first_grad, val_first_grad], axis=-1), "tm")
    width = key_first_grad.shape[-1]

    dims = (((2,), (1,)), ((), ()))
    first_rows = split_dot(first_sum[..., :width], w_key, dims)
    first_rows = first_rows + split_dot(first_sum[..., width:], w_value, dims)
    first_rows = jnp.where(is_owner, first_rows, jnp.zeros_like(first_rows))
    first_flat = normed_first.reshape(-1, normed_first.shape[-1])
    extra_key = split_dot(key_first_grad.reshape(-1, width), first_flat, (((0,), (0,)), ((), ()))).T
    extra_val = split_dot(val_first_grad.reshape(-1, width), first_flat, (((0,), (0,)), ((), ()))).T
    grad_normed = grad_normed.at[:, 0].add(first_rows)
    grad_wq = gram_rows(normed, grad_queries)
    grad_wk = gram_rows(normed, key_b) + extra_key
    grad_wv = gram_rows(normed, val_b) + extra_val
    grad_gain = jnp.sum(grad_normed * x_hat, axis=(0, 1, 2))
    grad_hat = grad_normed * norm_gain
    grad_x = inv_std * (
        grad_hat
        - jnp.mean(grad_hat, axis=-1, keepdims=True)
        - x_hat * jnp.mean(grad_hat * x_hat, axis=-1, keepdims=True)
    )
    grad_input = (grad_hidden.astype(jnp.float32) + grad_x).astype(jnp.bfloat16)
    grad_wq, grad_wk, grad_wv, grad_out, grad_gain = scatter_sum(
        (grad_wq, grad_wk, grad_wv, grad_out, grad_gain), "batch", "tm"
    )
    return (output, grad_input, grad_wq, grad_wk, grad_wv, grad_out, grad_gain)


def solution(mesh):
    in_specs = (
        P("batch", "tm", None, None),
        P(),
        P(),
        P(),
        P(),
        P(),
        P(),
        P("batch", "tm", None, None),
    )
    out_specs = (
        P("batch", "tm", None, None),
        P("batch", "tm", None, None),
        P(("batch", "tm"), None),
        P(("batch", "tm"), None),
        P(("batch", "tm"), None),
        P(("batch", "tm"), None),
        P(("batch", "tm")),
    )
    return jax.shard_map(
        on_device, mesh=mesh, in_specs=in_specs, out_specs=out_specs, check_vma=False
    )
```

```python
import functools

import jax
import jax.numpy as jnp
from jax import lax
from jax.sharding import PartitionSpec as P

HEADS = 10
HD = 64


eps_norm = 1e-05


def from_owner(block, axis):
    index = lax.axis_index(axis)
    have = block
    for target in range(1, lax.axis_size(axis)):
        got = lax.ppermute(block, axis, [(0, target)])
        have = jnp.where(index == target, got, have)
    return have


def to_owner(block, axis):
    total = block
    for source in range(1, lax.axis_size(axis)):
        got = lax.ppermute(block.astype(jnp.bfloat16), axis, [(source, 0)])
        total = total + got.astype(jnp.float32)
    return total


def scatter_sum(parts, outer, inner):
    count = lax.axis_size(outer) * lax.axis_size(inner)
    packed = jnp.concatenate([p.astype(jnp.bfloat16).reshape(count, -1) for p in parts], axis=1)
    share = packed.reshape((lax.axis_size(outer), -1) + packed.shape[1:])
    share = lax.psum_scatter(share, outer, scatter_dimension=0, tiled=True)[0]
    share = lax.all_to_all(share.astype(jnp.float32), inner, 0, 0, tiled=True)
    share = jnp.sum(share, axis=0)
    outs, start = [], 0
    for p in parts:
        width = p.size // count
        outs.append(share[start : start + width].reshape((p.shape[0] // count,) + p.shape[1:]))
        start += width
    return outs


def gain_sum(value, outer, inner):
    share = value.reshape(lax.axis_size(outer), lax.axis_size(inner), -1)
    share = jnp.sum(lax.all_to_all(share, outer, 0, 0, tiled=True), axis=0)
    return jnp.sum(lax.all_to_all(share, inner, 0, 0, tiled=True), axis=0)


def split_dot(wide, narrow, dims):
    high = wide.astype(jnp.bfloat16)
    low = (wide - high.astype(jnp.float32)).astype(jnp.bfloat16)
    return sum(
        lax.dot_general(part, narrow, dims, preferred_element_type=jnp.float32)
        for part in (high, low)
    )


def padded_2(value, sides, width):
    for axis, dim in sides:
        size, length = (lax.axis_size(axis), value.shape[dim])
        up = [(i, (i + 1) % size) for i in range(size - 1)]
        down = [(j, i) for i, j in up]
        last = lax.slice_in_dim(value, length - width, length, axis=dim)
        leading = lax.slice_in_dim(value, 0, width, axis=dim)
        before = lax.ppermute(last, axis, up)
        after = lax.ppermute(leading, axis, down)
        value = jnp.concatenate([before, value, after], axis=dim)
    return value


def layer_norm(inputs, norm_gain):
    wide = inputs.astype(jnp.float32)
    centre = jnp.mean(wide, axis=-1, keepdims=True)
    spread = jnp.mean((wide - centre) ** 2, axis=-1, keepdims=True)
    inv_std = lax.rsqrt(spread + eps_norm)
    x_hat = (wide - centre) * inv_std
    return ((x_hat * norm_gain).astype(jnp.bfloat16), x_hat, inv_std)


def project(inputs, matrix):
    return jnp.dot(inputs, matrix, preferred_element_type=jnp.float32).astype(jnp.bfloat16)


def split_heads(tensor):
    return tensor.reshape(tensor.shape[:-1] + (HEADS, HD))


def attend(queries, key_rows, val_rows, key_first, val_first):
    key_all = jnp.concatenate(
        [key_rows, jnp.broadcast_to(key_first[:, None], key_rows.shape)], axis=2
    )
    val_all = jnp.concatenate(
        [val_rows, jnp.broadcast_to(val_first[:, None], val_rows.shape)], axis=2
    )
    scores = jnp.einsum(
        "lfshd,lfthd->lfhst",
        split_heads(queries),
        split_heads(key_all),
        preferred_element_type=jnp.float32,
    ) * HD ** (-0.5)
    top_score = jnp.max(scores, axis=-1, keepdims=True)
    expd = jnp.exp(scores - top_score)
    prob_f32 = expd / jnp.sum(expd, axis=-1, keepdims=True)
    prob_b = lax.optimization_barrier(prob_f32.astype(jnp.bfloat16))
    mixed = jnp.einsum(
        "lfhst,lfthd->lfshd", prob_b, split_heads(val_all), preferred_element_type=jnp.float32
    )
    attended = mixed.reshape(queries.shape).astype(jnp.bfloat16)
    return (attended, prob_f32, prob_b, key_all, val_all)


def attend_back(grad_att, queries, key_all, val_all, prob_f32, prob_b):
    grad_heads = split_heads(grad_att)
    grad_prob = jnp.einsum(
        "lfshd,lfthd->lfhst", grad_heads, split_heads(val_all), preferred_element_type=jnp.float32
    )
    centre = jnp.sum(grad_prob * prob_f32, axis=-1, keepdims=True)
    grad_score = (prob_f32 * (grad_prob - centre) * HD ** (-0.5)).astype(jnp.bfloat16)
    grad_score = lax.optimization_barrier(grad_score)
    grad_queries = jnp.einsum(
        "lfhst,lfthd->lfshd", grad_score, split_heads(key_all), preferred_element_type=jnp.float32
    )
    grad_queries = grad_queries.reshape(queries.shape).astype(jnp.bfloat16)
    grad_keys = jnp.einsum(
        "lfhst,lfshd->lfthd", grad_score, split_heads(queries), preferred_element_type=jnp.float32
    ).reshape(key_all.shape)
    grad_vals = jnp.einsum(
        "lfhst,lfshd->lfthd", prob_b, grad_heads, preferred_element_type=jnp.float32
    ).reshape(val_all.shape)
    frame_len = queries.shape[2]
    return (
        grad_queries,
        grad_keys[:, :, :frame_len],
        grad_vals[:, :, :frame_len],
        jnp.sum(grad_keys[:, :, frame_len:], axis=1),
        jnp.sum(grad_vals[:, :, frame_len:], axis=1),
    )


def gram_rows(left, right, precision=None):
    flat_left = left.reshape(-1, left.shape[-1])
    flat_right = right.reshape(-1, right.shape[-1])
    return lax.dot_general(
        flat_left,
        flat_right,
        (((0,), (0,)), ((), ())),
        preferred_element_type=jnp.float32,
        precision=precision,
    )


def silu_slope(hidden_wide):
    sigma = jax.nn.sigmoid(hidden_wide)
    return sigma * (1.0 + hidden_wide * (1.0 - sigma))


def time_stack(padded, frames):
    return jnp.stack(
        [padded[:, 0:frames], padded[:, 1 : frames + 1], padded[:, 2 : frames + 2]], axis=3
    )


def on_device(x_in, norm_gain, w_query, w_key, w_value, w_out, w_time, cotangent):
    frames = x_in.shape[1]
    is_owner = lax.axis_index("tm") == 0
    normed, x_hat, inv_std = layer_norm(x_in, norm_gain)
    queries = project(normed, w_query)
    key_rows = project(normed, w_key)
    val_rows = project(normed, w_value)
    x_first = from_owner(x_in[:, 0], "tm")
    normed_first = layer_norm(x_first, norm_gain)[0]
    key_first = project(normed_first, w_key)
    val_first = project(normed_first, w_value)
    attended, prob_f32, prob_b, key_all, val_all = attend(
        queries, key_rows, val_rows, key_first, val_first
    )
    hidden = (
        x_in.astype(jnp.float32) + jnp.dot(attended, w_out, preferred_element_type=jnp.float32)
    ).astype(jnp.bfloat16)
    active = jax.nn.silu(hidden.astype(jnp.float32)).astype(jnp.bfloat16)
    grad_pad = padded_2(cotangent, (("tm", 1),), 1)
    act_stack = time_stack(padded_2(active, (("tm", 1),), 1), frames)
    conv = jnp.einsum("lfsjc,cjo->lfso", act_stack, w_time, preferred_element_type=jnp.float32)
    output = (hidden.astype(jnp.float32) + conv).astype(jnp.bfloat16)
    grad_stack = jnp.stack(
        [grad_pad[:, 2 : frames + 2], grad_pad[:, 1 : frames + 1], grad_pad[:, 0:frames]], axis=3
    )
    grad_act = jnp.einsum("lfsjo,cjo->lfsc", grad_stack, w_time, preferred_element_type=jnp.float32)
    grad_hidden = (
        cotangent.astype(jnp.float32) + grad_act * silu_slope(hidden.astype(jnp.float32))
    ).astype(jnp.bfloat16)
    grad_out = gram_rows(attended, grad_hidden)
    grad_att = jnp.einsum(
        "lfso,ho->lfsh", grad_hidden, w_out, preferred_element_type=jnp.float32
    ).astype(jnp.bfloat16)
    grad_queries, key_own, val_own, key_first_grad, val_first_grad = attend_back(
        grad_att, queries, key_all, val_all, prob_f32, prob_b
    )
    key_b = key_own.astype(jnp.bfloat16)
    val_b = val_own.astype(jnp.bfloat16)
    grad_normed = jnp.einsum(
        "lfsh,ch->lfsc", grad_queries, w_query, preferred_element_type=jnp.float32
    )
    grad_normed = grad_normed + jnp.einsum(
        "lfsh,ch->lfsc", key_b, w_key, preferred_element_type=jnp.float32
    )
    grad_normed = grad_normed + jnp.einsum(
        "lfsh,ch->lfsc", val_b, w_value, preferred_element_type=jnp.float32
    )
    first_sum = to_owner(jnp.concatenate([key_first_grad, val_first_grad], axis=-1), "tm")
    width = key_first_grad.shape[-1]

    dims = (((2,), (1,)), ((), ()))
    first_rows = split_dot(first_sum[..., :width], w_key, dims)
    first_rows = first_rows + split_dot(first_sum[..., width:], w_value, dims)
    first_rows = jnp.where(is_owner, first_rows, jnp.zeros_like(first_rows))
    first_flat = normed_first.reshape(-1, normed_first.shape[-1])
    extra_key = split_dot(key_first_grad.reshape(-1, width), first_flat, (((0,), (0,)), ((), ()))).T
    extra_val = split_dot(val_first_grad.reshape(-1, width), first_flat, (((0,), (0,)), ((), ()))).T
    grad_normed = grad_normed.at[:, 0].add(first_rows)
    grad_wq = gram_rows(normed, grad_queries)
    grad_wk = gram_rows(normed, key_b) + extra_key
    grad_wv = gram_rows(normed, val_b) + extra_val
    grad_gain = jnp.sum(grad_normed * x_hat, axis=(0, 1, 2))
    grad_hat = grad_normed * norm_gain
    grad_x = inv_std * (
        grad_hat
        - jnp.mean(grad_hat, axis=-1, keepdims=True)
        - x_hat * jnp.mean(grad_hat * x_hat, axis=-1, keepdims=True)
    )
    grad_input = (grad_hidden.astype(jnp.float32) + grad_x).astype(jnp.bfloat16)
    grad_wq, grad_wk, grad_wv, grad_out = scatter_sum(
        (grad_wq, grad_wk, grad_wv, grad_out), "batch", "tm"
    )
    grad_gain = gain_sum(grad_gain, "batch", "tm")
    return (output, grad_input, grad_wq, grad_wk, grad_wv, grad_out, grad_gain)


def solution(mesh):
    in_specs = (
        P("batch", "tm", None, None),
        P(),
        P(),
        P(),
        P(),
        P(),
        P(),
        P("batch", "tm", None, None),
    )
    out_specs = (
        P("batch", "tm", None, None),
        P("batch", "tm", None, None),
        P(("batch", "tm"), None),
        P(("batch", "tm"), None),
        P(("batch", "tm"), None),
        P(("batch", "tm"), None),
        P(("batch", "tm")),
    )
    return jax.shard_map(
        on_device, mesh=mesh, in_specs=in_specs, out_specs=out_specs, check_vma=False
    )
```

```python
import functools

import jax
import jax.numpy as jnp
from jax import lax
from jax.sharding import PartitionSpec as P

HEADS = 10
HD = 64


eps_norm = 1e-05


def from_owner(block, axis):
    index = lax.axis_index(axis)
    have = block
    for target in range(1, lax.axis_size(axis)):
        got = lax.ppermute(block, axis, [(0, target)])
        have = jnp.where(index == target, got, have)
    return have


def to_owner(block, axis):
    total = block
    for source in range(1, lax.axis_size(axis)):
        got = lax.ppermute(block.astype(jnp.bfloat16), axis, [(source, 0)])
        total = total + got.astype(jnp.float32)
    return total


def scatter_sum(parts, outer, inner):
    count = lax.axis_size(outer) * lax.axis_size(inner)
    packed = jnp.concatenate([p.astype(jnp.bfloat16).reshape(count, -1) for p in parts], axis=1)
    share = packed.reshape((lax.axis_size(outer), -1) + packed.shape[1:])
    share = lax.psum_scatter(share, outer, scatter_dimension=0, tiled=True)[0]
    share = lax.all_to_all(share, inner, 0, 0, tiled=True)
    share = jnp.sum(share.astype(jnp.float32), axis=0)
    outs, start = [], 0
    for p in parts:
        width = p.size // count
        outs.append(share[start : start + width].reshape((p.shape[0] // count,) + p.shape[1:]))
        start += width
    return outs


def gain_sum(value, outer, inner):
    share = value.reshape(lax.axis_size(outer), lax.axis_size(inner), -1)
    share = jnp.sum(lax.all_to_all(share, outer, 0, 0, tiled=True), axis=0)
    return jnp.sum(lax.all_to_all(share, inner, 0, 0, tiled=True), axis=0)


def split_dot(wide, narrow, dims):
    high = wide.astype(jnp.bfloat16)
    low = (wide - high.astype(jnp.float32)).astype(jnp.bfloat16)
    return sum(
        lax.dot_general(part, narrow, dims, preferred_element_type=jnp.float32)
        for part in (high, low)
    )


def padded_2(value, sides, width):
    for axis, dim in sides:
        size, length = (lax.axis_size(axis), value.shape[dim])
        up = [(i, (i + 1) % size) for i in range(size - 1)]
        down = [(j, i) for i, j in up]
        last = lax.slice_in_dim(value, length - width, length, axis=dim)
        leading = lax.slice_in_dim(value, 0, width, axis=dim)
        before = lax.ppermute(last, axis, up)
        after = lax.ppermute(leading, axis, down)
        value = jnp.concatenate([before, value, after], axis=dim)
    return value


def layer_norm(inputs, norm_gain):
    wide = inputs.astype(jnp.float32)
    centre = jnp.mean(wide, axis=-1, keepdims=True)
    spread = jnp.mean((wide - centre) ** 2, axis=-1, keepdims=True)
    inv_std = lax.rsqrt(spread + eps_norm)
    x_hat = (wide - centre) * inv_std
    return ((x_hat * norm_gain).astype(jnp.bfloat16), x_hat, inv_std)


def project(inputs, matrix):
    return jnp.dot(inputs, matrix, preferred_element_type=jnp.float32).astype(jnp.bfloat16)


def split_heads(tensor):
    return tensor.reshape(tensor.shape[:-1] + (HEADS, HD))


def attend(queries, key_rows, val_rows, key_first, val_first):
    key_all = jnp.concatenate(
        [key_rows, jnp.broadcast_to(key_first[:, None], key_rows.shape)], axis=2
    )
    val_all = jnp.concatenate(
        [val_rows, jnp.broadcast_to(val_first[:, None], val_rows.shape)], axis=2
    )
    scores = jnp.einsum(
        "lfshd,lfthd->lfhst",
        split_heads(queries),
        split_heads(key_all),
        preferred_element_type=jnp.float32,
    ) * HD ** (-0.5)
    top_score = jnp.max(scores, axis=-1, keepdims=True)
    expd = jnp.exp(scores - top_score)
    prob_f32 = expd / jnp.sum(expd, axis=-1, keepdims=True)
    prob_b = lax.optimization_barrier(prob_f32.astype(jnp.bfloat16))
    mixed = jnp.einsum(
        "lfhst,lfthd->lfshd", prob_b, split_heads(val_all), preferred_element_type=jnp.float32
    )
    attended = mixed.reshape(queries.shape).astype(jnp.bfloat16)
    return (attended, prob_f32, prob_b, key_all, val_all)


def attend_back(grad_att, queries, key_all, val_all, prob_f32, prob_b):
    grad_heads = split_heads(grad_att)
    grad_prob = jnp.einsum(
        "lfshd,lfthd->lfhst", grad_heads, split_heads(val_all), preferred_element_type=jnp.float32
    )
    centre = jnp.sum(grad_prob * prob_f32, axis=-1, keepdims=True)
    grad_score = (prob_f32 * (grad_prob - centre) * HD ** (-0.5)).astype(jnp.bfloat16)
    grad_score = lax.optimization_barrier(grad_score)
    grad_queries = jnp.einsum(
        "lfhst,lfthd->lfshd", grad_score, split_heads(key_all), preferred_element_type=jnp.float32
    )
    grad_queries = grad_queries.reshape(queries.shape).astype(jnp.bfloat16)
    grad_keys = jnp.einsum(
        "lfhst,lfshd->lfthd", grad_score, split_heads(queries), preferred_element_type=jnp.float32
    ).reshape(key_all.shape)
    grad_vals = jnp.einsum(
        "lfhst,lfshd->lfthd", prob_b, grad_heads, preferred_element_type=jnp.float32
    ).reshape(val_all.shape)
    frame_len = queries.shape[2]
    return (
        grad_queries,
        grad_keys[:, :, :frame_len],
        grad_vals[:, :, :frame_len],
        jnp.sum(grad_keys[:, :, frame_len:], axis=1),
        jnp.sum(grad_vals[:, :, frame_len:], axis=1),
    )


def gram_rows(left, right, precision=None):
    flat_left = left.reshape(-1, left.shape[-1])
    flat_right = right.reshape(-1, right.shape[-1])
    return lax.dot_general(
        flat_left,
        flat_right,
        (((0,), (0,)), ((), ())),
        preferred_element_type=jnp.float32,
        precision=precision,
    )


def silu_slope(hidden_wide):
    sigma = jax.nn.sigmoid(hidden_wide)
    return sigma * (1.0 + hidden_wide * (1.0 - sigma))


def time_stack(padded, frames):
    return jnp.stack(
        [padded[:, 0:frames], padded[:, 1 : frames + 1], padded[:, 2 : frames + 2]], axis=3
    )


def on_device(x_in, norm_gain, w_query, w_key, w_value, w_out, w_time, cotangent):
    frames = x_in.shape[1]
    is_owner = lax.axis_index("tm") == 0
    normed, x_hat, inv_std = layer_norm(x_in, norm_gain)
    queries = project(normed, w_query)
    key_rows = project(normed, w_key)
    val_rows = project(normed, w_value)
    x_first = from_owner(x_in[:, 0], "tm")
    normed_first = layer_norm(x_first, norm_gain)[0]
    key_first = project(normed_first, w_key)
    val_first = project(normed_first, w_value)
    attended, prob_f32, prob_b, key_all, val_all = attend(
        queries, key_rows, val_rows, key_first, val_first
    )
    hidden = (
        x_in.astype(jnp.float32) + jnp.dot(attended, w_out, preferred_element_type=jnp.float32)
    ).astype(jnp.bfloat16)
    active = jax.nn.silu(hidden.astype(jnp.float32)).astype(jnp.bfloat16)
    grad_pad = padded_2(cotangent, (("tm", 1),), 1)
    act_stack = time_stack(padded_2(active, (("tm", 1),), 1), frames)
    conv = jnp.einsum("lfsjc,cjo->lfso", act_stack, w_time, preferred_element_type=jnp.float32)
    output = (hidden.astype(jnp.float32) + conv).astype(jnp.bfloat16)
    grad_stack = jnp.stack(
        [grad_pad[:, 2 : frames + 2], grad_pad[:, 1 : frames + 1], grad_pad[:, 0:frames]], axis=3
    )
    grad_act = jnp.einsum("lfsjo,cjo->lfsc", grad_stack, w_time, preferred_element_type=jnp.float32)
    grad_hidden = (
        cotangent.astype(jnp.float32) + grad_act * silu_slope(hidden.astype(jnp.float32))
    ).astype(jnp.bfloat16)
    grad_out = gram_rows(attended, grad_hidden)
    grad_att = jnp.einsum(
        "lfso,ho->lfsh", grad_hidden, w_out, preferred_element_type=jnp.float32
    ).astype(jnp.bfloat16)
    grad_queries, key_own, val_own, key_first_grad, val_first_grad = attend_back(
        grad_att, queries, key_all, val_all, prob_f32, prob_b
    )
    key_b = key_own.astype(jnp.bfloat16)
    val_b = val_own.astype(jnp.bfloat16)
    grad_normed = jnp.einsum(
        "lfsh,ch->lfsc", grad_queries, w_query, preferred_element_type=jnp.float32
    )
    grad_normed = grad_normed + jnp.einsum(
        "lfsh,ch->lfsc", key_b, w_key, preferred_element_type=jnp.float32
    )
    grad_normed = grad_normed + jnp.einsum(
        "lfsh,ch->lfsc", val_b, w_value, preferred_element_type=jnp.float32
    )
    first_sum = to_owner(jnp.concatenate([key_first_grad, val_first_grad], axis=-1), "tm")
    width = key_first_grad.shape[-1]

    dims = (((2,), (1,)), ((), ()))
    first_rows = split_dot(first_sum[..., :width], w_key, dims)
    first_rows = first_rows + split_dot(first_sum[..., width:], w_value, dims)
    first_rows = jnp.where(is_owner, first_rows, jnp.zeros_like(first_rows))
    first_flat = normed_first.reshape(-1, normed_first.shape[-1])
    extra_key = split_dot(key_first_grad.reshape(-1, width), first_flat, (((0,), (0,)), ((), ()))).T
    extra_val = split_dot(val_first_grad.reshape(-1, width), first_flat, (((0,), (0,)), ((), ()))).T
    grad_normed = grad_normed.at[:, 0].add(first_rows)
    grad_wq = gram_rows(normed, grad_queries)
    grad_wk = gram_rows(normed, key_b) + extra_key
    grad_wv = gram_rows(normed, val_b) + extra_val
    grad_gain = jnp.sum(grad_normed * x_hat, axis=(0, 1, 2))
    grad_hat = grad_normed * norm_gain
    grad_x = inv_std * (
        grad_hat
        - jnp.mean(grad_hat, axis=-1, keepdims=True)
        - x_hat * jnp.mean(grad_hat * x_hat, axis=-1, keepdims=True)
    )
    grad_input = (grad_hidden.astype(jnp.float32) + grad_x).astype(jnp.bfloat16)
    grad_wq, grad_wk, grad_wv, grad_out = scatter_sum(
        (grad_wq, grad_wk, grad_wv, grad_out), "batch", "tm"
    )
    grad_gain = gain_sum(grad_gain, "batch", "tm")
    return (output, grad_input, grad_wq, grad_wk, grad_wv, grad_out, grad_gain)


def solution(mesh):
    in_specs = (
        P("batch", "tm", None, None),
        P(),
        P(),
        P(),
        P(),
        P(),
        P(),
        P("batch", "tm", None, None),
    )
    out_specs = (
        P("batch", "tm", None, None),
        P("batch", "tm", None, None),
        P(("batch", "tm"), None),
        P(("batch", "tm"), None),
        P(("batch", "tm"), None),
        P(("batch", "tm"), None),
        P(("batch", "tm")),
    )
    return jax.shard_map(
        on_device, mesh=mesh, in_specs=in_specs, out_specs=out_specs, check_vma=False
    )
```

```python
import functools

import jax
import jax.numpy as jnp
from jax import lax
from jax.sharding import PartitionSpec as P

HEADS = 10
HD = 64


eps_norm = 1e-05


def from_owner(block, axis):
    index = lax.axis_index(axis)
    have = block
    for target in range(1, lax.axis_size(axis)):
        got = lax.ppermute(block, axis, [(0, target)])
        have = jnp.where(index == target, got, have)
    return have


def to_owner(block, axis):
    total = block
    for source in range(1, lax.axis_size(axis)):
        got = lax.ppermute(block.astype(jnp.bfloat16), axis, [(source, 0)])
        total = total + got.astype(jnp.float32)
    return total


def scatter_sum(parts, outer, inner):
    count = lax.axis_size(outer) * lax.axis_size(inner)
    packed = jnp.concatenate([p.astype(jnp.bfloat16).reshape(count, -1) for p in parts], axis=1)
    share = packed.reshape((lax.axis_size(outer), -1) + packed.shape[1:])
    share = lax.psum_scatter(share, outer, scatter_dimension=0, tiled=True)[0]
    share = lax.all_to_all(share, inner, 0, 0, tiled=True)
    share = jnp.sum(share.astype(jnp.float32), axis=0)
    outs, start = [], 0
    for p in parts:
        width = p.size // count
        outs.append(share[start : start + width].reshape((p.shape[0] // count,) + p.shape[1:]))
        start += width
    return outs


def gain_sum(value, outer, inner):
    share = value.reshape(lax.axis_size(outer), lax.axis_size(inner), -1)
    share = jnp.sum(lax.all_to_all(share, outer, 0, 0, tiled=True), axis=0)
    return jnp.sum(lax.all_to_all(share, inner, 0, 0, tiled=True), axis=0)


def split_dot(wide, narrow, dims):
    high = wide.astype(jnp.bfloat16)
    low = (wide - high.astype(jnp.float32)).astype(jnp.bfloat16)
    return sum(
        lax.dot_general(part, narrow, dims, preferred_element_type=jnp.float32)
        for part in (high, low)
    )


def padded_2(value, sides, width):
    for axis, dim in sides:
        size, length = (lax.axis_size(axis), value.shape[dim])
        up = [(i, (i + 1) % size) for i in range(size - 1)]
        down = [(j, i) for i, j in up]
        last = lax.slice_in_dim(value, length - width, length, axis=dim)
        leading = lax.slice_in_dim(value, 0, width, axis=dim)
        before = lax.ppermute(last, axis, up)
        after = lax.ppermute(leading, axis, down)
        value = jnp.concatenate([before, value, after], axis=dim)
    return value


def layer_norm(inputs, norm_gain):
    wide = inputs.astype(jnp.float32)
    centre = jnp.mean(wide, axis=-1, keepdims=True)
    spread = jnp.mean((wide - centre) ** 2, axis=-1, keepdims=True)
    inv_std = lax.rsqrt(spread + eps_norm)
    x_hat = (wide - centre) * inv_std
    return ((x_hat * norm_gain).astype(jnp.bfloat16), x_hat, inv_std)


def project(inputs, matrix):
    return jnp.dot(inputs, matrix, preferred_element_type=jnp.float32).astype(jnp.bfloat16)


def split_heads(tensor):
    return tensor.reshape(tensor.shape[:-1] + (HEADS, HD))


def attend(queries, key_rows, val_rows, key_first, val_first):
    key_all = jnp.concatenate(
        [key_rows, jnp.broadcast_to(key_first[:, None], key_rows.shape)], axis=2
    )
    val_all = jnp.concatenate(
        [val_rows, jnp.broadcast_to(val_first[:, None], val_rows.shape)], axis=2
    )
    scores = jnp.einsum(
        "lfshd,lfthd->lfhst",
        split_heads(queries),
        split_heads(key_all),
        preferred_element_type=jnp.float32,
    ) * HD ** (-0.5)
    top_score = jnp.max(scores, axis=-1, keepdims=True)
    expd = jnp.exp(scores - top_score)
    prob_f32 = expd / jnp.sum(expd, axis=-1, keepdims=True)
    prob_b = lax.optimization_barrier(prob_f32.astype(jnp.bfloat16))
    mixed = jnp.einsum(
        "lfhst,lfthd->lfshd", prob_b, split_heads(val_all), preferred_element_type=jnp.float32
    )
    attended = mixed.reshape(queries.shape).astype(jnp.bfloat16)
    return (attended, prob_f32, prob_b, key_all, val_all)


def attend_back(grad_att, queries, key_all, val_all, prob_f32, prob_b):
    grad_heads = split_heads(grad_att)
    grad_prob = jnp.einsum(
        "lfshd,lfthd->lfhst", grad_heads, split_heads(val_all), preferred_element_type=jnp.float32
    )
    centre = jnp.sum(grad_prob * prob_f32, axis=-1, keepdims=True)
    grad_score = (prob_f32 * (grad_prob - centre) * HD ** (-0.5)).astype(jnp.bfloat16)
    grad_score = lax.optimization_barrier(grad_score)
    grad_queries = jnp.einsum(
        "lfhst,lfthd->lfshd", grad_score, split_heads(key_all), preferred_element_type=jnp.float32
    )
    grad_queries = grad_queries.reshape(queries.shape).astype(jnp.bfloat16)
    grad_keys = jnp.einsum(
        "lfhst,lfshd->lfthd", grad_score, split_heads(queries), preferred_element_type=jnp.float32
    ).reshape(key_all.shape)
    grad_vals = jnp.einsum(
        "lfhst,lfshd->lfthd", prob_b, grad_heads, preferred_element_type=jnp.float32
    ).reshape(val_all.shape)
    frame_len = queries.shape[2]
    return (
        grad_queries,
        grad_keys[:, :, :frame_len],
        grad_vals[:, :, :frame_len],
        jnp.sum(grad_keys[:, :, frame_len:], axis=1),
        jnp.sum(grad_vals[:, :, frame_len:], axis=1),
    )


def gram_rows(left, right, precision=None):
    flat_left = left.reshape(-1, left.shape[-1])
    flat_right = right.reshape(-1, right.shape[-1])
    return lax.dot_general(
        flat_left,
        flat_right,
        (((0,), (0,)), ((), ())),
        preferred_element_type=jnp.float32,
        precision=precision,
    )


def silu_slope(hidden_wide):
    sigma = jax.nn.sigmoid(hidden_wide)
    return sigma * (1.0 + hidden_wide * (1.0 - sigma))


def time_stack(padded, frames):
    return jnp.stack(
        [padded[:, 0:frames], padded[:, 1 : frames + 1], padded[:, 2 : frames + 2]], axis=3
    )


def on_device(x_in, norm_gain, w_query, w_key, w_value, w_out, w_time, cotangent):
    frames = x_in.shape[1]
    is_owner = lax.axis_index("tm") == 0
    normed, x_hat, inv_std = layer_norm(x_in, norm_gain)
    queries = project(normed, w_query)
    key_rows = project(normed, w_key)
    val_rows = project(normed, w_value)
    x_first = from_owner(x_in[:, 0], "tm")
    normed_first = layer_norm(x_first, norm_gain)[0]
    key_first = project(normed_first, w_key)
    val_first = project(normed_first, w_value)
    attended, prob_f32, prob_b, key_all, val_all = attend(
        queries, key_rows, val_rows, key_first, val_first
    )
    hidden = (
        x_in.astype(jnp.float32) + jnp.dot(attended, w_out, preferred_element_type=jnp.float32)
    ).astype(jnp.bfloat16)
    active = jax.nn.silu(hidden.astype(jnp.float32)).astype(jnp.bfloat16)
    grad_pad = padded_2(cotangent, (("tm", 1),), 1)
    act_stack = time_stack(padded_2(active, (("tm", 1),), 1), frames)
    conv = jnp.einsum("lfsjc,cjo->lfso", act_stack, w_time, preferred_element_type=jnp.float32)
    output = (hidden.astype(jnp.float32) + conv).astype(jnp.bfloat16)
    grad_stack = jnp.stack(
        [grad_pad[:, 2 : frames + 2], grad_pad[:, 1 : frames + 1], grad_pad[:, 0:frames]], axis=3
    )
    grad_act = jnp.einsum("lfsjo,cjo->lfsc", grad_stack, w_time, preferred_element_type=jnp.float32)
    grad_hidden = (
        cotangent.astype(jnp.float32) + grad_act * silu_slope(hidden.astype(jnp.float32))
    ).astype(jnp.bfloat16)
    grad_out = gram_rows(attended, grad_hidden)
    grad_att = jnp.einsum(
        "lfso,ho->lfsh", grad_hidden, w_out, preferred_element_type=jnp.float32
    ).astype(jnp.bfloat16)
    grad_queries, key_own, val_own, key_first_grad, val_first_grad = attend_back(
        grad_att, queries, key_all, val_all, prob_f32, prob_b
    )
    key_b = key_own.astype(jnp.bfloat16)
    val_b = val_own.astype(jnp.bfloat16)
    grad_normed = jnp.einsum(
        "lfsh,ch->lfsc", grad_queries, w_query, preferred_element_type=jnp.float32
    )
    grad_normed = grad_normed + jnp.einsum(
        "lfsh,ch->lfsc", key_b, w_key, preferred_element_type=jnp.float32
    )
    grad_normed = grad_normed + jnp.einsum(
        "lfsh,ch->lfsc", val_b, w_value, preferred_element_type=jnp.float32
    )
    first_sum = to_owner(jnp.concatenate([key_first_grad, val_first_grad], axis=-1), "tm")
    width = key_first_grad.shape[-1]

    first_flat = normed_first.reshape(-1, normed_first.shape[-1])
    extra_key = split_dot(key_first_grad.reshape(-1, width), first_flat, (((0,), (0,)), ((), ()))).T
    extra_val = split_dot(val_first_grad.reshape(-1, width), first_flat, (((0,), (0,)), ((), ()))).T
    grad_wq = gram_rows(normed, grad_queries)
    grad_wk = gram_rows(normed, key_b) + extra_key
    grad_wv = gram_rows(normed, val_b) + extra_val
    grad_wq, grad_wk, grad_wv, grad_out, first_sum = lax.optimization_barrier(
        (grad_wq, grad_wk, grad_wv, grad_out, first_sum)
    )
    dims = (((2,), (1,)), ((), ()))
    first_rows = split_dot(first_sum[..., :width], w_key, dims)
    first_rows = first_rows + split_dot(first_sum[..., width:], w_value, dims)
    first_rows = jnp.where(is_owner, first_rows, jnp.zeros_like(first_rows))
    grad_normed = grad_normed.at[:, 0].add(first_rows)
    grad_gain = jnp.sum(grad_normed * x_hat, axis=(0, 1, 2))
    grad_hat = grad_normed * norm_gain
    grad_x = inv_std * (
        grad_hat
        - jnp.mean(grad_hat, axis=-1, keepdims=True)
        - x_hat * jnp.mean(grad_hat * x_hat, axis=-1, keepdims=True)
    )
    grad_input = (grad_hidden.astype(jnp.float32) + grad_x).astype(jnp.bfloat16)
    grad_wq, grad_wk, grad_wv, grad_out = scatter_sum(
        (grad_wq, grad_wk, grad_wv, grad_out), "batch", "tm"
    )
    grad_gain = gain_sum(grad_gain, "batch", "tm")
    return (output, grad_input, grad_wq, grad_wk, grad_wv, grad_out, grad_gain)


def solution(mesh):
    in_specs = (
        P("batch", "tm", None, None),
        P(),
        P(),
        P(),
        P(),
        P(),
        P(),
        P("batch", "tm", None, None),
    )
    out_specs = (
        P("batch", "tm", None, None),
        P("batch", "tm", None, None),
        P(("batch", "tm"), None),
        P(("batch", "tm"), None),
        P(("batch", "tm"), None),
        P(("batch", "tm"), None),
        P(("batch", "tm")),
    )
    return jax.shard_map(
        on_device, mesh=mesh, in_specs=in_specs, out_specs=out_specs, check_vma=False
    )
```

```python
import functools

import jax
import jax.numpy as jnp
from jax import lax
from jax.sharding import PartitionSpec as P

HEADS = 10
HD = 64


eps_norm = 1e-05


def from_owner(block, axis):
    index = lax.axis_index(axis)
    have = block
    for target in range(1, lax.axis_size(axis)):
        got = lax.ppermute(block, axis, [(0, target)])
        have = jnp.where(index == target, got, have)
    return have


def to_owner(block, axis):
    total = block
    for source in range(1, lax.axis_size(axis)):
        got = lax.ppermute(block.astype(jnp.bfloat16), axis, [(source, 0)])
        total = total + got.astype(jnp.float32)
    return total


def scatter_sum(parts, outer, inner):
    count = lax.axis_size(outer) * lax.axis_size(inner)
    packed = jnp.concatenate([p.astype(jnp.bfloat16).reshape(count, -1) for p in parts], axis=1)
    share = packed.reshape((lax.axis_size(outer), -1) + packed.shape[1:])
    share = lax.psum_scatter(share, outer, scatter_dimension=0, tiled=True)[0]
    share = lax.all_to_all(share, inner, 0, 0, tiled=True)
    share = jnp.sum(share.astype(jnp.float32), axis=0)
    outs, start = [], 0
    for p in parts:
        width = p.size // count
        outs.append(share[start : start + width].reshape((p.shape[0] // count,) + p.shape[1:]))
        start += width
    return outs


def gain_sum(value, outer, inner):
    share = value.reshape(lax.axis_size(outer), lax.axis_size(inner), -1)
    share = jnp.sum(lax.all_to_all(share, outer, 0, 0, tiled=True), axis=0)
    return jnp.sum(lax.all_to_all(share, inner, 0, 0, tiled=True), axis=0)


def split_dot(wide, narrow, dims):
    high = wide.astype(jnp.bfloat16)
    low = (wide - high.astype(jnp.float32)).astype(jnp.bfloat16)
    return sum(
        lax.dot_general(part, narrow, dims, preferred_element_type=jnp.float32)
        for part in (high, low)
    )


def padded_2(value, sides, width):
    for axis, dim in sides:
        size, length = (lax.axis_size(axis), value.shape[dim])
        up = [(i, (i + 1) % size) for i in range(size - 1)]
        down = [(j, i) for i, j in up]
        last = lax.slice_in_dim(value, length - width, length, axis=dim)
        leading = lax.slice_in_dim(value, 0, width, axis=dim)
        before = lax.ppermute(last, axis, up)
        after = lax.ppermute(leading, axis, down)
        value = jnp.concatenate([before, value, after], axis=dim)
    return value


def layer_norm(inputs, norm_gain):
    wide = inputs.astype(jnp.float32)
    centre = jnp.mean(wide, axis=-1, keepdims=True)
    spread = jnp.mean((wide - centre) ** 2, axis=-1, keepdims=True)
    inv_std = lax.rsqrt(spread + eps_norm)
    x_hat = (wide - centre) * inv_std
    return ((x_hat * norm_gain).astype(jnp.bfloat16), x_hat, inv_std)


def project(inputs, matrix):
    return jnp.dot(inputs, matrix, preferred_element_type=jnp.float32).astype(jnp.bfloat16)


def split_heads(tensor):
    return tensor.reshape(tensor.shape[:-1] + (HEADS, HD))


def attend(queries, key_rows, val_rows, key_first, val_first):
    key_all = jnp.concatenate(
        [key_rows, jnp.broadcast_to(key_first[:, None], key_rows.shape)], axis=2
    )
    val_all = jnp.concatenate(
        [val_rows, jnp.broadcast_to(val_first[:, None], val_rows.shape)], axis=2
    )
    scores = jnp.einsum(
        "lfshd,lfthd->lfhst",
        split_heads(queries),
        split_heads(key_all),
        preferred_element_type=jnp.float32,
    ) * HD ** (-0.5)
    top_score = jnp.max(scores, axis=-1, keepdims=True)
    expd = jnp.exp(scores - top_score)
    prob_f32 = expd / jnp.sum(expd, axis=-1, keepdims=True)
    prob_b = lax.optimization_barrier(prob_f32.astype(jnp.bfloat16))
    mixed = jnp.einsum(
        "lfhst,lfthd->lfshd", prob_b, split_heads(val_all), preferred_element_type=jnp.float32
    )
    attended = mixed.reshape(queries.shape).astype(jnp.bfloat16)
    return (attended, prob_f32, prob_b, key_all, val_all)


def attend_back(grad_att, queries, key_all, val_all, prob_f32, prob_b):
    grad_heads = split_heads(grad_att)
    grad_prob = jnp.einsum(
        "lfshd,lfthd->lfhst", grad_heads, split_heads(val_all), preferred_element_type=jnp.float32
    )
    centre = jnp.sum(grad_prob * prob_f32, axis=-1, keepdims=True)
    grad_score = (prob_f32 * (grad_prob - centre) * HD ** (-0.5)).astype(jnp.bfloat16)
    grad_score = lax.optimization_barrier(grad_score)
    grad_queries = jnp.einsum(
        "lfhst,lfthd->lfshd", grad_score, split_heads(key_all), preferred_element_type=jnp.float32
    )
    grad_queries = grad_queries.reshape(queries.shape).astype(jnp.bfloat16)
    grad_keys = jnp.einsum(
        "lfhst,lfshd->lfthd", grad_score, split_heads(queries), preferred_element_type=jnp.float32
    ).reshape(key_all.shape)
    grad_vals = jnp.einsum(
        "lfhst,lfshd->lfthd", prob_b, grad_heads, preferred_element_type=jnp.float32
    ).reshape(val_all.shape)
    frame_len = queries.shape[2]
    return (
        grad_queries,
        grad_keys[:, :, :frame_len],
        grad_vals[:, :, :frame_len],
        jnp.sum(grad_keys[:, :, frame_len:], axis=1),
        jnp.sum(grad_vals[:, :, frame_len:], axis=1),
    )


def gram_rows(left, right, precision=None):
    flat_left = left.reshape(-1, left.shape[-1])
    flat_right = right.reshape(-1, right.shape[-1])
    return lax.dot_general(
        flat_left,
        flat_right,
        (((0,), (0,)), ((), ())),
        preferred_element_type=jnp.float32,
        precision=precision,
    )


def silu_slope(hidden_wide):
    sigma = jax.nn.sigmoid(hidden_wide)
    return sigma * (1.0 + hidden_wide * (1.0 - sigma))


def time_stack(padded, frames):
    return jnp.stack(
        [padded[:, 0:frames], padded[:, 1 : frames + 1], padded[:, 2 : frames + 2]], axis=3
    )


def on_device(x_in, norm_gain, w_query, w_key, w_value, w_out, w_time, cotangent):
    frames = x_in.shape[1]
    is_owner = lax.axis_index("tm") == 0
    normed, x_hat, inv_std = layer_norm(x_in, norm_gain)
    queries = project(normed, w_query)
    key_rows = project(normed, w_key)
    val_rows = project(normed, w_value)
    x_first = from_owner(x_in[:, 0], "tm")
    normed_first = layer_norm(x_first, norm_gain)[0]
    key_first = project(normed_first, w_key)
    val_first = project(normed_first, w_value)
    attended, prob_f32, prob_b, key_all, val_all = attend(
        queries, key_rows, val_rows, key_first, val_first
    )
    hidden = (
        x_in.astype(jnp.float32) + jnp.dot(attended, w_out, preferred_element_type=jnp.float32)
    ).astype(jnp.bfloat16)
    active = jax.nn.silu(hidden.astype(jnp.float32)).astype(jnp.bfloat16)
    grad_pad = padded_2(cotangent, (("tm", 1),), 1)
    act_stack = time_stack(padded_2(active, (("tm", 1),), 1), frames)
    conv = jnp.einsum("lfsjc,cjo->lfso", act_stack, w_time, preferred_element_type=jnp.float32)
    output = (hidden.astype(jnp.float32) + conv).astype(jnp.bfloat16)
    grad_stack = jnp.stack(
        [grad_pad[:, 2 : frames + 2], grad_pad[:, 1 : frames + 1], grad_pad[:, 0:frames]], axis=3
    )
    grad_act = jnp.einsum("lfsjo,cjo->lfsc", grad_stack, w_time, preferred_element_type=jnp.float32)
    grad_hidden = (
        cotangent.astype(jnp.float32) + grad_act * silu_slope(hidden.astype(jnp.float32))
    ).astype(jnp.bfloat16)
    grad_out = gram_rows(attended, grad_hidden)
    grad_att = jnp.einsum(
        "lfso,ho->lfsh", grad_hidden, w_out, preferred_element_type=jnp.float32
    ).astype(jnp.bfloat16)
    grad_queries, key_own, val_own, key_first_grad, val_first_grad = attend_back(
        grad_att, queries, key_all, val_all, prob_f32, prob_b
    )
    key_b = key_own.astype(jnp.bfloat16)
    val_b = val_own.astype(jnp.bfloat16)
    grad_normed = jnp.einsum(
        "lfsh,ch->lfsc", grad_queries, w_query, preferred_element_type=jnp.float32
    )
    grad_normed = grad_normed + jnp.einsum(
        "lfsh,ch->lfsc", key_b, w_key, preferred_element_type=jnp.float32
    )
    grad_normed = grad_normed + jnp.einsum(
        "lfsh,ch->lfsc", val_b, w_value, preferred_element_type=jnp.float32
    )
    first_sum = to_owner(jnp.concatenate([key_first_grad, val_first_grad], axis=-1), "tm")
    width = key_first_grad.shape[-1]

    dims = (((2,), (1,)), ((), ()))
    first_rows = split_dot(first_sum[..., :width], w_key, dims)
    first_rows = first_rows + split_dot(first_sum[..., width:], w_value, dims)
    first_rows = jnp.where(is_owner, first_rows, jnp.zeros_like(first_rows))
    first_flat = normed_first.reshape(-1, normed_first.shape[-1])
    grad_normed = grad_normed.at[:, 0].add(first_rows)
    own = jnp.concatenate([grad_queries, key_b, val_b], axis=-1).reshape(-1, 3 * width)
    first_grads = jnp.concatenate([key_first_grad, val_first_grad], axis=-1).reshape(-1, 2 * width)
    first_high = first_grads.astype(jnp.bfloat16)
    first_low = (first_grads - first_high.astype(jnp.float32)).astype(jnp.bfloat16)
    blank = jnp.zeros((first_grads.shape[0], width), jnp.bfloat16)
    rhs = jnp.concatenate(
        [
            own,
            jnp.concatenate([blank, first_high], axis=-1),
            jnp.concatenate([blank, first_low], axis=-1),
        ],
        axis=0,
    )
    lhs = jnp.concatenate([normed.reshape(-1, normed.shape[-1]), first_flat, first_flat], axis=0)
    grad_qkv = gram_rows(lhs, rhs)
    grad_gain = jnp.sum(grad_normed * x_hat, axis=(0, 1, 2))
    grad_hat = grad_normed * norm_gain
    grad_x = inv_std * (
        grad_hat
        - jnp.mean(grad_hat, axis=-1, keepdims=True)
        - x_hat * jnp.mean(grad_hat * x_hat, axis=-1, keepdims=True)
    )
    grad_input = (grad_hidden.astype(jnp.float32) + grad_x).astype(jnp.bfloat16)
    grad_qkv, grad_out = scatter_sum((grad_qkv, grad_out), "batch", "tm")
    grad_wq, grad_wk, grad_wv = jnp.split(grad_qkv, 3, axis=-1)
    grad_gain = gain_sum(grad_gain, "batch", "tm")
    return (output, grad_input, grad_wq, grad_wk, grad_wv, grad_out, grad_gain)


def solution(mesh):
    in_specs = (
        P("batch", "tm", None, None),
        P(),
        P(),
        P(),
        P(),
        P(),
        P(),
        P("batch", "tm", None, None),
    )
    out_specs = (
        P("batch", "tm", None, None),
        P("batch", "tm", None, None),
        P(("batch", "tm"), None),
        P(("batch", "tm"), None),
        P(("batch", "tm"), None),
        P(("batch", "tm"), None),
        P(("batch", "tm")),
    )
    return jax.shard_map(
        on_device, mesh=mesh, in_specs=in_specs, out_specs=out_specs, check_vma=False
    )
```
